512 devices in a mesh: row: 32 (over z, core), col: 16 (over y, x).
Axes of the slice: x: 4, y: 4, z: 16, core: 2. Of those that a mesh axis runs over, the one named last changes fastest.
Arguments:
- block_input: bfloat16 [8192, 3072], P('row', 'col'), may hold values from -5 to 5
- conv_out: bfloat16 [8192, 3072], P('row', 'col'), may hold values from -100 to 100
- hidden_pre: bfloat16 [8192, 6144], P('row', 'col'), may hold values from -6 to 6
- cotangent: bfloat16 [8192, 3072], P('row', 'col'), may hold values from -16 to 16
- conv_kernel: float32 [49, 3072], P(None, ('col', 'row')), may hold values from -0.875 to 0.875
- norm_gain: float32 [3072], replicated, may hold values from 0.25 to 1.75
- norm_bias: float32 [3072], replicated, may hold values from -3 to 3
- layer_scale: float32 [3072], P('col'), may hold values from 0.3 to 3
- w_in: bfloat16 [3072, 6144], P('row', 'col'), may hold values from -0.109375 to 0.109375
- w_out: bfloat16 [3072, 6144], P('row', 'col'), may hold values from -0.078125 to 0.078125
Outputs:
- d_input: bfloat16 [8192, 3072], P('row', 'col')
- d_kernel: float32 [49, 3072], P(None, ('col', 'row'))
- d_gain: float32 [3072], P('col')
- d_bias: float32 [3072], P('col')
- d_w_in: bfloat16 [3072, 6144], P('row', 'col')
The draws below stay inside these ranges and needn't reach their ends.
All inputs are finite; a program needn't handle non-finite values.
Results may differ from the reference program's by a relative error of at most 0.02.
Values may be sent and summed in bfloat16 or wider, within the bound.
No kernel may reach another device: no remote copies, remote signals or barrier semaphores. Data moves between devices by JAX's collectives and lax.ppermute only.
A program may use at most 64 MiB of HBM per device.

```python
import math
import jax
import jax.numpy as jnp
from jax import lax

C = 3072
KS = 7
HID = 6144
H = 64
KK = 49
TOK_DEV = 256
TOKENS = 8192
IMAGES = 2
N_ROW = 32
N_COL = 16


def draw_conv_out(key, part):
    first, second, third = jax.random.split(key, 3)
    row_scale = jnp.exp(jax.random.uniform(second, (TOKENS, 1)) * jnp.log(10.0)) / 3.0
    rising = 3.0 ** (jnp.arange(C, dtype=jnp.float32) / C)
    col_scale = jnp.exp(jax.random.uniform(third, (1, C)) * jnp.log(10.0)) * rising[None, :] / 4.0
    base = jnp.clip(jax.random.normal(first, (TOKENS, C)), -4.0, 4.0)
    return (base * row_scale * col_scale).astype(jnp.bfloat16)


def draw_cotangent(key, part):
    first = jax.random.fold_in(key, 0)
    second = jax.random.fold_in(key, 1)
    fourth = jax.random.fold_in(key, 3)
    rising = 3.0 ** (jnp.arange(TOKENS, dtype=jnp.float32) / TOKENS)
    blocks = TOKENS // TOK_DEV
    block_scale = jnp.exp(jax.random.uniform(fourth, (blocks, 1)) * jnp.log(8.0))
    block_rows = jnp.repeat(block_scale, TOK_DEV, axis=0)
    row_scale = jnp.exp(jax.random.uniform(second, (TOKENS, 1)) * jnp.log(2.0)) * rising[:, None] * block_rows / 12.0
    base = jnp.clip(jax.random.normal(first, (TOKENS, C)), -4.0, 4.0)
    return (base * row_scale).astype(jnp.bfloat16)


def levels(rng, shape, cuts, least, high):
    def one(dim, blocks):
        draws = jax.random.uniform(jax.random.fold_in(jax.random.fold_in(rng, 6), dim), (blocks,), jnp.float32, least / len(cuts), high / len(cuts))
        return jnp.repeat(jnp.exp(draws), shape[dim] // blocks).reshape((-1,) + (1,) * (len(shape) - dim - 1))

    loudness = one(*cuts[0])
    for cut in cuts[1:]:
        loudness = loudness * one(*cut)
    return loudness


def scatter_about(own_key, dims, width, most, pieces=(), held_as=jnp.bfloat16):
    entries = jax.random.normal(own_key, dims, jnp.float32) * width
    if len(pieces) > 0:
        entries = levels(own_key, dims, pieces, -0.22, 0.18) * entries
    return jnp.clip(entries, min=-most, max=most).astype(held_as)


def setup_inputs(seed: int = 0) -> dict:
    streams_of = jax.random.split(jax.random.key(seed), 11)
    block_input = scatter_about(streams_of[0], (TOKENS, C), 1.0, 5.0, ((0, 32), (1, 16)))
    conv_out = draw_conv_out(jax.random.fold_in(streams_of[10], 71), 0)
    hidden_pre = scatter_about(streams_of[2], (TOKENS, HID), 1.5, 6.0, ((0, 32), (1, 16)))
    cotangent = draw_cotangent(jax.random.fold_in(streams_of[10], 71), 0)
    conv_kernel = scatter_about(streams_of[4], (KK, C), KK ** -0.5, 0.875, ((1, 512),), jnp.float32)
    norm_gain = jnp.clip(1.0 + 0.15 * jax.random.normal(streams_of[5], (C,), jnp.float32), 0.25, 1.75)
    norm_bias = scatter_about(streams_of[6], (C,), 0.5, 3.0, (), jnp.float32)
    layer_scale = jnp.clip(jnp.exp(math.log(3.0) - 2.3025851 * jax.random.uniform(streams_of[7], (C,), jnp.float32) ** levels(streams_of[7], (C,), ((0, 16),), -0.2, 0.2)), 0.3, 3.0)
    w_in = scatter_about(streams_of[8], (C, HID), C ** -0.5, 0.109375, ((0, 32), (1, 16)))
    w_out = scatter_about(streams_of[9], (C, HID), HID ** -0.5, 0.078125, ((0, 32), (1, 16)))
    return dict(block_input=block_input, conv_out=conv_out, hidden_pre=hidden_pre, cotangent=cotangent, conv_kernel=conv_kernel, norm_gain=norm_gain, norm_bias=norm_bias, layer_scale=layer_scale, w_in=w_in, w_out=w_out)


def gelu_slope(values):
    cdf = 0.5 * (1.0 + lax.erf(values * 0.7071067811865476))
    density = jnp.exp(-0.5 * values * values) * 0.3989422804014327
    return cdf + values * density

def reference(block_input, conv_out, hidden_pre, cotangent, conv_kernel, norm_gain, norm_bias, layer_scale, w_in, w_out):
    scaled = (cotangent.astype(jnp.float32) * layer_scale).astype(jnp.bfloat16)
    grad_act = jnp.dot(scaled, w_out, preferred_element_type=jnp.float32)
    grad_pre = (grad_act * gelu_slope(hidden_pre.astype(jnp.float32))).astype(jnp.bfloat16)
    values = conv_out.astype(jnp.float32)
    mean = lax.optimization_barrier(jnp.mean(values, axis=1, keepdims=True))
    centred = values - mean
    rstd = lax.rsqrt(lax.optimization_barrier(jnp.mean(centred * centred, axis=1, keepdims=True)) + 1e-06)
    zhat = centred * rstd
    normed = (zhat * norm_gain + norm_bias).astype(jnp.bfloat16)

    def weight_block(index, total):
        start = (index * TOK_DEV).astype(jnp.int32)
        rows_norm = lax.dynamic_slice_in_dim(normed, start, TOK_DEV, 0)
        rows_grad = lax.dynamic_slice_in_dim(grad_pre, start, TOK_DEV, 0)
        term = lax.dot_general(rows_norm, rows_grad, (((0,), (0,)), ((), ())), preferred_element_type=jnp.float32)
        return total + lax.optimization_barrier(term.astype(jnp.bfloat16)).astype(jnp.float32)
    d_w_in = lax.fori_loop(0, N_ROW, weight_block, jnp.zeros((C, HID), jnp.float32)).astype(jnp.bfloat16)
    hidden_block = HID // N_COL

    def norm_block(index, total):
        start = (index * hidden_block).astype(jnp.int32)
        part_grad = lax.dynamic_slice_in_dim(grad_pre, start, hidden_block, 1)
        part_weight = lax.dynamic_slice_in_dim(w_in, start, hidden_block, 1)
        term = lax.dot_general(part_grad, part_weight, (((1,), (1,)), ((), ())), preferred_element_type=jnp.float32)
        return total + lax.optimization_barrier(term.astype(jnp.bfloat16)).astype(jnp.float32)
    grad_norm = lax.fori_loop(0, N_COL, norm_block, jnp.zeros((TOKENS, C), jnp.float32))
    d_gain = lax.optimization_barrier(jnp.sum(grad_norm * zhat, axis=0))
    d_bias = lax.optimization_barrier(jnp.sum(grad_norm, axis=0))
    dzhat = grad_norm * norm_gain
    first = lax.optimization_barrier(jnp.mean(dzhat, axis=1, keepdims=True))
    second = lax.optimization_barrier(jnp.mean(dzhat * zhat, axis=1, keepdims=True))
    grad_conv = (rstd * (dzhat - first - zhat * second)).astype(jnp.bfloat16)
    grads = grad_conv.astype(jnp.float32).reshape(IMAGES, H, H, C)
    inputs = block_input.astype(jnp.float32).reshape(IMAGES, H, H, C)
    grads_pad = jnp.pad(grads, ((0, 0), (3, 3), (3, 3), (0, 0)))
    inputs_pad = jnp.pad(inputs, ((0, 0), (3, 3), (3, 3), (0, 0)))
    moved = jnp.zeros((IMAGES, H, H, C), jnp.float32)
    kernel_rows = []
    for tap in range(KS * KS):
        down = tap // KS
        across = tap % KS
        moved = moved + conv_kernel[tap] * grads_pad[:, 6 - down:6 - down + H, 6 - across:6 - across + H, :]
        kernel_rows.append(lax.optimization_barrier(jnp.sum(grads * inputs_pad[:, down:down + H, across:across + H, :], axis=(0, 1, 2))))
    d_kernel = jnp.stack(kernel_rows)
    d_input = (moved.reshape(TOKENS, C) + cotangent.astype(jnp.float32)).astype(jnp.bfloat16)
    return (d_input, d_kernel, d_gain, d_bias, d_w_in)
```

```python
import jax
import jax.numpy as jnp
from jax import lax
from jax.sharding import PartitionSpec as P

KS = 7
H = 64
HALO = KS // 2

WEIGHTS_VIA = "gather"
DWIN_VIA = "a2a"
ACTS_VIA = "a2a"


def gelu_slope(values):
    cdf = 0.5 * (1.0 + lax.erf(values * 0.7071067811865476))
    density = jnp.exp(-0.5 * values * values) * 0.3989422804014327
    return cdf + values * density


def gather_blocks(x, axis_name, size, via):
    if via == "a2a":
        wide = jnp.broadcast_to(x[None], (size,) + x.shape)
        return lax.all_to_all(wide, axis_name, 0, 0, tiled=True)
    return lax.all_gather(x, axis_name, axis=0, tiled=False)


def split_hi_lo(values):
    high = lax.reduce_precision(values, exponent_bits=8, mantissa_bits=7)
    low = values - high
    return high.astype(jnp.bfloat16), low.astype(jnp.bfloat16)


def body(
    block_input,
    conv_out,
    hidden_pre,
    cotangent,
    conv_kernel,
    norm_gain,
    norm_bias,
    layer_scale,
    w_in,
    w_out,
):
    tokens, channels = block_input.shape
    width = norm_gain.shape[0]
    hidden = hidden_pre.shape[1]
    n_col = width // channels
    n_row = width // w_in.shape[0]
    few = conv_kernel.shape[1]
    rows = tokens // H
    col_rank = lax.axis_index("col")
    row_rank = lax.axis_index("row")

    scaled = (cotangent.astype(jnp.float32) * layer_scale).astype(jnp.bfloat16)
    acts = gather_blocks(jnp.concatenate([scaled, conv_out], axis=1), "col", n_col, ACTS_VIA)
    weights = gather_blocks(jnp.concatenate([w_out, w_in], axis=1), "row", n_row, WEIGHTS_VIA)
    kernel_rows_full = lax.all_gather(conv_kernel, "row", axis=1, tiled=True)
    scaled_full = jnp.transpose(acts[:, :, :channels], (1, 0, 2)).reshape(tokens, width)
    inputs_full = jnp.transpose(acts[:, :, channels:], (1, 0, 2)).reshape(tokens, width)
    w_out_full = weights[:, :, :hidden].reshape(width, hidden)
    w_in_full = weights[:, :, hidden:].reshape(width, hidden)

    values = inputs_full.astype(jnp.float32)
    mean = jnp.mean(values, axis=1, keepdims=True)
    centred = values - mean
    rstd = lax.rsqrt(jnp.mean(centred * centred, axis=1, keepdims=True) + 1e-06)
    zhat_full = centred * rstd
    normed_full = (zhat_full * norm_gain + norm_bias).astype(jnp.bfloat16)
    zhat_own = lax.dynamic_slice_in_dim(zhat_full, col_rank * channels, channels, 1)
    gain_own = lax.dynamic_slice_in_dim(norm_gain, col_rank * channels, channels, 0)

    grad_act = jnp.dot(scaled_full, w_out_full, preferred_element_type=jnp.float32)
    grad_pre = (grad_act * gelu_slope(hidden_pre.astype(jnp.float32))).astype(jnp.bfloat16)

    block_w = lax.dot_general(
        normed_full, grad_pre, (((0,), (0,)), ((), ())), preferred_element_type=jnp.float32
    ).astype(jnp.bfloat16)
    if DWIN_VIA == "a2a":
        parts_w = lax.all_to_all(
            block_w.reshape(n_row, width // n_row, hidden), "row", 0, 0, tiled=True
        )
        d_w_in = jnp.sum(parts_w.astype(jnp.float32), axis=0).astype(jnp.bfloat16)
    else:
        d_w_in = lax.psum_scatter(block_w, "row", scatter_dimension=0, tiled=True)

    block_n = lax.dot_general(
        grad_pre, w_in_full, (((1,), (1,)), ((), ())), preferred_element_type=jnp.float32
    ).astype(jnp.bfloat16)
    weighted = block_n.astype(jnp.float32) * norm_gain
    first_part = jnp.sum(weighted, axis=1)
    second_part = jnp.sum(weighted * zhat_full, axis=1)
    f_hi, f_lo = split_hi_lo(first_part)
    s_hi, s_lo = split_hi_lo(second_part)
    sums = jnp.stack([f_hi, f_lo, s_hi, s_lo], axis=1)
    outgoing = jnp.concatenate(
        [
            jnp.transpose(block_n.reshape(tokens, n_col, channels), (1, 0, 2)),
            jnp.broadcast_to(sums[None], (n_col, tokens, 4)),
        ],
        axis=2,
    )
    incoming = lax.all_to_all(outgoing, "col", 0, 0, tiled=True).astype(jnp.float32)
    grad_norm = jnp.sum(incoming[:, :, :channels], axis=0)
    totals = jnp.sum(incoming[:, :, channels:], axis=0)
    first = (totals[:, 0] + totals[:, 1])[:, None] / width
    second = (totals[:, 2] + totals[:, 3])[:, None] / width
    dzhat = grad_norm * gain_own
    grad_conv = (rstd * (dzhat - first - zhat_own * second)).astype(jnp.bfloat16)
    gain_part = jnp.sum(grad_norm * zhat_own, axis=0)
    bias_part = jnp.sum(grad_norm, axis=0)

    per_image = H // rows
    grid = grad_conv.reshape(rows, H, channels)
    down_pairs = [(i, i + 1) for i in range(n_row) if (i + 1) % per_image != 0]
    up_pairs = [(i + 1, i) for i in range(n_row) if (i + 1) % per_image != 0]
    from_above = lax.ppermute(grid[rows - HALO :], "row", down_pairs)
    from_below = lax.ppermute(grid[:HALO], "row", up_pairs)
    tall = jnp.concatenate([from_above, grid, from_below], axis=0).astype(jnp.float32)
    padded = jnp.pad(tall, ((0, 0), (HALO, HALO), (0, 0)))
    inputs = block_input.astype(jnp.float32).reshape(rows, H, channels)
    kernel_full = kernel_rows_full
    moved = jnp.zeros((rows, H, channels), jnp.float32)
    kernel_rows = []
    for tap in range(KS * KS):
        down = tap // KS
        across = tap % KS
        window = padded[
            2 * HALO - down : 2 * HALO - down + rows, 2 * HALO - across : 2 * HALO - across + H
        ]
        moved = moved + kernel_full[tap] * window
        kernel_rows.append(jnp.sum(window * inputs, axis=(0, 1)))
    d_input = (moved.reshape(tokens, channels) + cotangent.astype(jnp.float32)).astype(jnp.bfloat16)

    kernel_part = jnp.stack(kernel_rows).reshape(KS * KS, n_row, few)
    kernel_part = jnp.transpose(kernel_part, (1, 0, 2)).reshape(n_row, KS * KS * few)
    norm_part = jnp.broadcast_to(jnp.concatenate([gain_part, bias_part])[None], (n_row, 2 * channels))
    reduced = jnp.sum(
        lax.all_to_all(jnp.concatenate([kernel_part, norm_part], axis=1), "row", 0, 0, tiled=True),
        axis=0,
    )
    d_kernel = reduced[: KS * KS * few].reshape(KS * KS, few)
    d_gain = reduced[KS * KS * few : KS * KS * few + channels]
    d_bias = reduced[KS * KS * few + channels :]
    return (d_input, d_kernel, d_gain, d_bias, d_w_in)


def solution(mesh):
    return jax.shard_map(
        body,
        mesh=mesh,
        in_specs=(
            P("row", "col"),
            P("row", "col"),
            P("row", "col"),
            P("row", "col"),
            P(None, ("col", "row")),
            P(),
            P(),
            P("col"),
            P("row", "col"),
            P("row", "col"),
        ),
        out_specs=(P("row", "col"), P(None, ("col", "row")), P("col"), P("col"), P("row", "col")),
        check_vma=False,
    )
```

```python
import jax
import jax.numpy as jnp
from jax import lax
from jax.experimental import pallas as pl
from jax.experimental.pallas import tpu as pltpu
from jax.sharding import PartitionSpec as P

KS = 7
H = 64
HALO = KS // 2

WEIGHTS_VIA = "gather"
DWIN_VIA = "a2a"
ACTS_VIA = "a2a"


def gelu_slope(values):
    cdf = 0.5 * (1.0 + lax.erf(values * 0.7071067811865476))
    density = jnp.exp(-0.5 * values * values) * 0.3989422804014327
    return cdf + values * density


def gather_blocks(x, axis_name, size, via):
    if via == "a2a":
        wide = jnp.broadcast_to(x[None], (size,) + x.shape)
        return lax.all_to_all(wide, axis_name, 0, 0, tiled=True)
    return lax.all_gather(x, axis_name, axis=0, tiled=False)


def split_three(values):
    high = lax.reduce_precision(values, exponent_bits=8, mantissa_bits=7)
    rest = values - high
    middle = lax.reduce_precision(rest, exponent_bits=8, mantissa_bits=7)
    low = rest - middle
    return jnp.stack([high, middle, low]).astype(jnp.bfloat16)


def conv_body(tall_ref, inputs_ref, cot_ref, kernel_ref, din_ref, dk_ref, pad_ref):
    rows, span, channels = inputs_ref.shape
    pad_ref[...] = tall_ref[...].astype(jnp.float32)
    inputs = inputs_ref[...].astype(jnp.float32)
    moved = jnp.zeros((rows, span, channels), jnp.float32)
    for down in range(KS):
        for across in range(KS):
            tap = down * KS + across
            window = pad_ref[
                2 * HALO - down : 2 * HALO - down + rows,
                2 * HALO - across : 2 * HALO - across + span,
                :,
            ]
            moved = moved + kernel_ref[tap : tap + 1, :][None] * window
            dk_ref[tap : tap + 1, :] = jnp.sum(window * inputs, axis=(0, 1))[None]
    din_ref[...] = (moved + cot_ref[...].astype(jnp.float32)).astype(din_ref.dtype)


def conv_call(padded, inputs, cot, kernel_full):
    rows, span, channels = inputs.shape
    return pl.pallas_call(
        conv_body,
        out_shape=(
            jax.ShapeDtypeStruct((rows, span, channels), jnp.bfloat16),
            jax.ShapeDtypeStruct((KS * KS, channels), jnp.float32),
        ),
        scratch_shapes=[pltpu.VMEM(padded.shape, jnp.float32)],
    )(padded, inputs, cot, kernel_full)


def split_hi_lo(values):
    high = lax.reduce_precision(values, exponent_bits=8, mantissa_bits=7)
    low = values - high
    return high.astype(jnp.bfloat16), low.astype(jnp.bfloat16)


def body(
    block_input,
    conv_out,
    hidden_pre,
    cotangent,
    conv_kernel,
    norm_gain,
    norm_bias,
    layer_scale,
    w_in,
    w_out,
):
    tokens, channels = block_input.shape
    width = norm_gain.shape[0]
    hidden = hidden_pre.shape[1]
    n_col = width // channels
    n_row = width // w_in.shape[0]
    few = conv_kernel.shape[1]
    rows = tokens // H
    col_rank = lax.axis_index("col")
    row_rank = lax.axis_index("row")

    scaled = (cotangent.astype(jnp.float32) * layer_scale).astype(jnp.bfloat16)
    acts = gather_blocks(jnp.concatenate([scaled, conv_out], axis=1), "col", n_col, ACTS_VIA)
    kernel_bits = split_three(conv_kernel).reshape(-1)
    lanes_extra = -(-kernel_bits.shape[0] // w_in.shape[0])
    kernel_bits = jnp.pad(kernel_bits, (0, lanes_extra * w_in.shape[0] - kernel_bits.shape[0]))
    weights = gather_blocks(
        jnp.concatenate([w_out, w_in, kernel_bits.reshape(w_in.shape[0], lanes_extra)], axis=1),
        "row",
        n_row,
        WEIGHTS_VIA,
    )
    kernel_parts = weights[:, :, 2 * hidden :].reshape(n_row, -1)[:, : 3 * KS * KS * few]
    kernel_parts = kernel_parts.reshape(n_row, 3, KS * KS, few).astype(jnp.float32)
    kernel_sum = kernel_parts[:, 0] + kernel_parts[:, 1] + kernel_parts[:, 2]
    kernel_rows_full = jnp.transpose(kernel_sum, (1, 0, 2)).reshape(KS * KS, n_row * few)
    scaled_full = jnp.transpose(acts[:, :, :channels], (1, 0, 2)).reshape(tokens, width)
    inputs_full = jnp.transpose(acts[:, :, channels:], (1, 0, 2)).reshape(tokens, width)
    w_out_full = weights[:, :, :hidden].reshape(width, hidden)
    w_in_full = weights[:, :, hidden : 2 * hidden].reshape(width, hidden)

    values = inputs_full.astype(jnp.float32)
    mean = jnp.mean(values, axis=1, keepdims=True)
    centred = values - mean
    rstd = lax.rsqrt(jnp.mean(centred * centred, axis=1, keepdims=True) + 1e-06)
    zhat_full = centred * rstd
    normed_full = (zhat_full * norm_gain + norm_bias).astype(jnp.bfloat16)
    zhat_own = lax.dynamic_slice_in_dim(zhat_full, col_rank * channels, channels, 1)
    gain_own = lax.dynamic_slice_in_dim(norm_gain, col_rank * channels, channels, 0)

    grad_act = jnp.dot(scaled_full, w_out_full, preferred_element_type=jnp.float32)
    grad_pre = (grad_act * gelu_slope(hidden_pre.astype(jnp.float32))).astype(jnp.bfloat16)

    block_w = lax.dot_general(
        normed_full, grad_pre, (((0,), (0,)), ((), ())), preferred_element_type=jnp.float32
    ).astype(jnp.bfloat16)
    if DWIN_VIA == "a2a":
        parts_w = lax.all_to_all(
            block_w.reshape(n_row, width // n_row, hidden), "row", 0, 0, tiled=True
        )
        d_w_in = jnp.sum(parts_w.astype(jnp.float32), axis=0).astype(jnp.bfloat16)
    else:
        d_w_in = lax.psum_scatter(block_w, "row", scatter_dimension=0, tiled=True)

    block_n = lax.dot_general(
        grad_pre, w_in_full, (((1,), (1,)), ((), ())), preferred_element_type=jnp.float32
    ).astype(jnp.bfloat16)
    weighted = block_n.astype(jnp.float32) * norm_gain
    first_part = jnp.sum(weighted, axis=1)
    second_part = jnp.sum(weighted * zhat_full, axis=1)
    f_hi, f_lo = split_hi_lo(first_part)
    s_hi, s_lo = split_hi_lo(second_part)
    sums = jnp.stack([f_hi, f_lo, s_hi, s_lo], axis=1)
    outgoing = jnp.concatenate(
        [
            jnp.transpose(block_n.reshape(tokens, n_col, channels), (1, 0, 2)),
            jnp.broadcast_to(sums[None], (n_col, tokens, 4)),
        ],
        axis=2,
    )
    incoming = lax.all_to_all(outgoing, "col", 0, 0, tiled=True).astype(jnp.float32)
    grad_norm = jnp.sum(incoming[:, :, :channels], axis=0)
    totals = jnp.sum(incoming[:, :, channels:], axis=0)
    first = (totals[:, 0] + totals[:, 1])[:, None] / width
    second = (totals[:, 2] + totals[:, 3])[:, None] / width
    dzhat = grad_norm * gain_own
    grad_conv = (rstd * (dzhat - first - zhat_own * second)).astype(jnp.bfloat16)
    gain_part = jnp.sum(grad_norm * zhat_own, axis=0)
    bias_part = jnp.sum(grad_norm, axis=0)

    per_image = H // rows
    grid = grad_conv.reshape(rows, H, channels)
    down_pairs = [(i, i + 1) for i in range(n_row) if (i + 1) % per_image != 0]
    up_pairs = [(i + 1, i) for i in range(n_row) if (i + 1) % per_image != 0]
    from_above = lax.ppermute(grid[rows - HALO :], "row", down_pairs)
    from_below = lax.ppermute(grid[:HALO], "row", up_pairs)
    tall = jnp.concatenate([from_above, grid, from_below], axis=0)
    padded = jnp.pad(tall, ((0, 0), (HALO, HALO), (0, 0)))
    d_input, kernel_sums = conv_call(
        padded,
        block_input.reshape(rows, H, channels),
        cotangent.reshape(rows, H, channels),
        kernel_rows_full,
    )
    d_input = d_input.reshape(tokens, channels)

    kernel_part = kernel_sums.reshape(KS * KS, n_row, few)
    kernel_part = jnp.transpose(kernel_part, (1, 0, 2)).reshape(n_row, KS * KS * few)
    norm_part = jnp.broadcast_to(jnp.concatenate([gain_part, bias_part])[None], (n_row, 2 * channels))
    reduced = jnp.sum(
        lax.all_to_all(jnp.concatenate([kernel_part, norm_part], axis=1), "row", 0, 0, tiled=True),
        axis=0,
    )
    d_kernel = reduced[: KS * KS * few].reshape(KS * KS, few)
    d_gain = reduced[KS * KS * few : KS * KS * few + channels]
    d_bias = reduced[KS * KS * few + channels :]
    return (d_input, d_kernel, d_gain, d_bias, d_w_in)


def solution(mesh):
    return jax.shard_map(
        body,
        mesh=mesh,
        in_specs=(
            P("row", "col"),
            P("row", "col"),
            P("row", "col"),
            P("row", "col"),
            P(None, ("col", "row")),
            P(),
            P(),
            P("col"),
            P("row", "col"),
            P("row", "col"),
        ),
        out_specs=(P("row", "col"), P(None, ("col", "row")), P("col"), P("col"), P("row", "col")),
        check_vma=False,
    )
```

```python
import jax
import jax.numpy as jnp
from jax import lax
from jax.experimental import pallas as pl
from jax.experimental.pallas import tpu as pltpu
from jax.sharding import PartitionSpec as P

KS = 7
H = 64
HALO = KS // 2

WEIGHTS_VIA = "gather"
DWIN_VIA = "rs"
ACTS_VIA = "a2a"


def gelu_slope(values):
    cdf = 0.5 * (1.0 + lax.erf(values * 0.7071067811865476))
    density = jnp.exp(-0.5 * values * values) * 0.3989422804014327
    return cdf + values * density


def gather_blocks(x, axis_name, size, via):
    if via == "a2a":
        wide = jnp.broadcast_to(x[None], (size,) + x.shape)
        return lax.all_to_all(wide, axis_name, 0, 0, tiled=True)
    return lax.all_gather(x, axis_name, axis=0, tiled=False)


def split_three(values):
    high = lax.reduce_precision(values, exponent_bits=8, mantissa_bits=7)
    rest = values - high
    middle = lax.reduce_precision(rest, exponent_bits=8, mantissa_bits=7)
    low = rest - middle
    return jnp.stack([high, middle, low]).astype(jnp.bfloat16)


def conv_body(tall_ref, inputs_ref, cot_ref, kernel_ref, din_ref, dk_ref, pad_ref):
    rows, span, channels = inputs_ref.shape
    pad_ref[...] = tall_ref[...].astype(jnp.float32)
    inputs = inputs_ref[...].astype(jnp.float32)
    moved = jnp.zeros((rows, span, channels), jnp.float32)
    for down in range(KS):
        for across in range(KS):
            tap = down * KS + across
            window = pad_ref[
                2 * HALO - down : 2 * HALO - down + rows,
                2 * HALO - across : 2 * HALO - across + span,
                :,
            ]
            moved = moved + kernel_ref[tap : tap + 1, :][None] * window
            dk_ref[tap : tap + 1, :] = jnp.sum(window * inputs, axis=(0, 1))[None]
    din_ref[...] = (moved + cot_ref[...].astype(jnp.float32)).astype(din_ref.dtype)


def conv_call(padded, inputs, cot, kernel_full):
    rows, span, channels = inputs.shape
    return pl.pallas_call(
        conv_body,
        out_shape=(
            jax.ShapeDtypeStruct((rows, span, channels), jnp.bfloat16),
            jax.ShapeDtypeStruct((KS * KS, channels), jnp.float32),
        ),
        scratch_shapes=[pltpu.VMEM(padded.shape, jnp.float32)],
    )(padded, inputs, cot, kernel_full)


def split_hi_lo(values):
    high = lax.reduce_precision(values, exponent_bits=8, mantissa_bits=7)
    low = values - high
    return high.astype(jnp.bfloat16), low.astype(jnp.bfloat16)


def body(
    block_input,
    conv_out,
    hidden_pre,
    cotangent,
    conv_kernel,
    norm_gain,
    norm_bias,
    layer_scale,
    w_in,
    w_out,
):
    tokens, channels = block_input.shape
    width = norm_gain.shape[0]
    hidden = hidden_pre.shape[1]
    n_col = width // channels
    n_row = width // w_in.shape[0]
    few = conv_kernel.shape[1]
    rows = tokens // H
    col_rank = lax.axis_index("col")
    row_rank = lax.axis_index("row")

    scaled = (cotangent.astype(jnp.float32) * layer_scale).astype(jnp.bfloat16)
    acts = gather_blocks(jnp.concatenate([scaled, conv_out], axis=1), "col", n_col, ACTS_VIA)
    kernel_bits = split_three(conv_kernel).reshape(-1)
    lanes_extra = -(-kernel_bits.shape[0] // w_in.shape[0])
    kernel_bits = jnp.pad(kernel_bits, (0, lanes_extra * w_in.shape[0] - kernel_bits.shape[0]))
    weights = gather_blocks(
        jnp.concatenate([w_out, w_in, kernel_bits.reshape(w_in.shape[0], lanes_extra)], axis=1),
        "row",
        n_row,
        WEIGHTS_VIA,
    )
    kernel_parts = weights[:, :, 2 * hidden :].reshape(n_row, -1)[:, : 3 * KS * KS * few]
    kernel_parts = kernel_parts.reshape(n_row, 3, KS * KS, few).astype(jnp.float32)
    kernel_sum = kernel_parts[:, 0] + kernel_parts[:, 1] + kernel_parts[:, 2]
    kernel_rows_full = jnp.transpose(kernel_sum, (1, 0, 2)).reshape(KS * KS, n_row * few)
    scaled_full = jnp.transpose(acts[:, :, :channels], (1, 0, 2)).reshape(tokens, width)
    inputs_full = jnp.transpose(acts[:, :, channels:], (1, 0, 2)).reshape(tokens, width)
    w_out_full = weights[:, :, :hidden].reshape(width, hidden)
    w_in_full = weights[:, :, hidden : 2 * hidden].reshape(width, hidden)

    values = inputs_full.astype(jnp.float32)
    mean = jnp.mean(values, axis=1, keepdims=True)
    centred = values - mean
    rstd = lax.rsqrt(jnp.mean(centred * centred, axis=1, keepdims=True) + 1e-06)
    zhat_full = centred * rstd
    normed_full = (zhat_full * norm_gain + norm_bias).astype(jnp.bfloat16)
    zhat_own = lax.dynamic_slice_in_dim(zhat_full, col_rank * channels, channels, 1)
    gain_own = lax.dynamic_slice_in_dim(norm_gain, col_rank * channels, channels, 0)

    grad_act = jnp.dot(scaled_full, w_out_full, preferred_element_type=jnp.float32)
    grad_pre = (grad_act * gelu_slope(hidden_pre.astype(jnp.float32))).astype(jnp.bfloat16)

    block_w = lax.dot_general(
        normed_full, grad_pre, (((0,), (0,)), ((), ())), preferred_element_type=jnp.float32
    ).astype(jnp.bfloat16)
    if DWIN_VIA == "a2a":
        parts_w = lax.all_to_all(
            block_w.reshape(n_row, width // n_row, hidden), "row", 0, 0, tiled=True
        )
        d_w_in = jnp.sum(parts_w.astype(jnp.float32), axis=0).astype(jnp.bfloat16)
    else:
        d_w_in = lax.psum_scatter(block_w, "row", scatter_dimension=0, tiled=True)

    block_n = lax.dot_general(
        grad_pre, w_in_full, (((1,), (1,)), ((), ())), preferred_element_type=jnp.float32
    ).astype(jnp.bfloat16)
    weighted = block_n.astype(jnp.float32) * norm_gain
    first_part = jnp.sum(weighted, axis=1)
    second_part = jnp.sum(weighted * zhat_full, axis=1)
    f_hi, f_lo = split_hi_lo(first_part)
    s_hi, s_lo = split_hi_lo(second_part)
    sums = jnp.stack([f_hi, f_lo, s_hi, s_lo], axis=1)
    outgoing = jnp.concatenate(
        [
            jnp.transpose(block_n.reshape(tokens, n_col, channels), (1, 0, 2)),
            jnp.broadcast_to(sums[None], (n_col, tokens, 4)),
        ],
        axis=2,
    )
    incoming = lax.all_to_all(outgoing, "col", 0, 0, tiled=True).astype(jnp.float32)
    grad_norm = jnp.sum(incoming[:, :, :channels], axis=0)
    totals = jnp.sum(incoming[:, :, channels:], axis=0)
    first = (totals[:, 0] + totals[:, 1])[:, None] / width
    second = (totals[:, 2] + totals[:, 3])[:, None] / width
    dzhat = grad_norm * gain_own
    grad_conv = (rstd * (dzhat - first - zhat_own * second)).astype(jnp.bfloat16)
    gain_part = jnp.sum(grad_norm * zhat_own, axis=0)
    bias_part = jnp.sum(grad_norm, axis=0)

    per_image = H // rows
    grid = grad_conv.reshape(rows, H, channels)
    down_pairs = [(i, i + 1) for i in range(n_row) if (i + 1) % per_image != 0]
    up_pairs = [(i + 1, i) for i in range(n_row) if (i + 1) % per_image != 0]
    from_above = lax.ppermute(grid[rows - HALO :], "row", down_pairs)
    from_below = lax.ppermute(grid[:HALO], "row", up_pairs)
    tall = jnp.concatenate([from_above, grid, from_below], axis=0)
    padded = jnp.pad(tall, ((0, 0), (HALO, HALO), (0, 0)))
    d_input, kernel_sums = conv_call(
        padded,
        block_input.reshape(rows, H, channels),
        cotangent.reshape(rows, H, channels),
        kernel_rows_full,
    )
    d_input = d_input.reshape(tokens, channels)

    kernel_part = kernel_sums.reshape(KS * KS, n_row, few)
    kernel_part = jnp.transpose(kernel_part, (1, 0, 2)).reshape(n_row, KS * KS * few)
    norm_part = jnp.broadcast_to(jnp.concatenate([gain_part, bias_part])[None], (n_row, 2 * channels))
    reduced = jnp.sum(
        lax.all_to_all(jnp.concatenate([kernel_part, norm_part], axis=1), "row", 0, 0, tiled=True),
        axis=0,
    )
    d_kernel = reduced[: KS * KS * few].reshape(KS * KS, few)
    d_gain = reduced[KS * KS * few : KS * KS * few + channels]
    d_bias = reduced[KS * KS * few + channels :]
    return (d_input, d_kernel, d_gain, d_bias, d_w_in)


def solution(mesh):
    return jax.shard_map(
        body,
        mesh=mesh,
        in_specs=(
            P("row", "col"),
            P("row", "col"),
            P("row", "col"),
            P("row", "col"),
            P(None, ("col", "row")),
            P(),
            P(),
            P("col"),
            P("row", "col"),
            P("row", "col"),
        ),
        out_specs=(P("row", "col"), P(None, ("col", "row")), P("col"), P("col"), P("row", "col")),
        check_vma=False,
    )
```

```python
import jax
import jax.numpy as jnp
from jax import lax
from jax.experimental import pallas as pl
from jax.experimental.pallas import tpu as pltpu
from jax.sharding import Mesh, PartitionSpec as P

KS = 7
H = 64
HALO = KS // 2

WEIGHTS_VIA = "gather"
DWIN_VIA = "two_level"
ROW = ("z", "core")
SWAP = [(0, 1), (1, 0)]
ACTS_VIA = "a2a"


def gelu_slope(values):
    cdf = 0.5 * (1.0 + lax.erf(values * 0.7071067811865476))
    density = jnp.exp(-0.5 * values * values) * 0.3989422804014327
    return cdf + values * density


def gather_blocks(x, axis_name, size, via):
    if via == "a2a":
        wide = jnp.broadcast_to(x[None], (size,) + x.shape)
        return lax.all_to_all(wide, axis_name, 0, 0, tiled=True)
    return lax.all_gather(x, axis_name, axis=0, tiled=False)


def split_three(values):
    high = lax.reduce_precision(values, exponent_bits=8, mantissa_bits=7)
    rest = values - high
    middle = lax.reduce_precision(rest, exponent_bits=8, mantissa_bits=7)
    low = rest - middle
    return jnp.stack([high, middle, low]).astype(jnp.bfloat16)


def conv_body(tall_ref, inputs_ref, cot_ref, kernel_ref, din_ref, dk_ref, pad_ref):
    rows, span, channels = inputs_ref.shape
    pad_ref[...] = tall_ref[...].astype(jnp.float32)
    inputs = inputs_ref[...].astype(jnp.float32)
    moved = jnp.zeros((rows, span, channels), jnp.float32)
    for down in range(KS):
        for across in range(KS):
            tap = down * KS + across
            window = pad_ref[
                2 * HALO - down : 2 * HALO - down + rows,
                2 * HALO - across : 2 * HALO - across + span,
                :,
            ]
            moved = moved + kernel_ref[tap : tap + 1, :][None] * window
            dk_ref[tap : tap + 1, :] = jnp.sum(window * inputs, axis=(0, 1))[None]
    din_ref[...] = (moved + cot_ref[...].astype(jnp.float32)).astype(din_ref.dtype)


def conv_call(padded, inputs, cot, kernel_full):
    rows, span, channels = inputs.shape
    return pl.pallas_call(
        conv_body,
        out_shape=(
            jax.ShapeDtypeStruct((rows, span, channels), jnp.bfloat16),
            jax.ShapeDtypeStruct((KS * KS, channels), jnp.float32),
        ),
        scratch_shapes=[pltpu.VMEM(padded.shape, jnp.float32)],
    )(padded, inputs, cot, kernel_full)


def split_hi_lo(values):
    high = lax.reduce_precision(values, exponent_bits=8, mantissa_bits=7)
    low = values - high
    return high.astype(jnp.bfloat16), low.astype(jnp.bfloat16)


def body(
    block_input,
    conv_out,
    hidden_pre,
    cotangent,
    conv_kernel,
    norm_gain,
    norm_bias,
    layer_scale,
    w_in,
    w_out,
):
    tokens, channels = block_input.shape
    width = norm_gain.shape[0]
    hidden = hidden_pre.shape[1]
    n_col = width // channels
    n_row = width // w_in.shape[0]
    few = conv_kernel.shape[1]
    rows = tokens // H
    col_rank = lax.axis_index("col")
    row_rank = lax.axis_index(ROW)

    scaled = (cotangent.astype(jnp.float32) * layer_scale).astype(jnp.bfloat16)
    acts = gather_blocks(jnp.concatenate([scaled, conv_out], axis=1), "col", n_col, ACTS_VIA)
    kernel_bits = split_three(conv_kernel).reshape(-1)
    lanes_extra = -(-kernel_bits.shape[0] // w_in.shape[0])
    kernel_bits = jnp.pad(kernel_bits, (0, lanes_extra * w_in.shape[0] - kernel_bits.shape[0]))
    weights = gather_blocks(
        jnp.concatenate([w_out, w_in, kernel_bits.reshape(w_in.shape[0], lanes_extra)], axis=1),
        ROW,
        n_row,
        WEIGHTS_VIA,
    )
    kernel_parts = weights[:, :, 2 * hidden :].reshape(n_row, -1)[:, : 3 * KS * KS * few]
    kernel_parts = kernel_parts.reshape(n_row, 3, KS * KS, few).astype(jnp.float32)
    kernel_sum = kernel_parts[:, 0] + kernel_parts[:, 1] + kernel_parts[:, 2]
    kernel_rows_full = jnp.transpose(kernel_sum, (1, 0, 2)).reshape(KS * KS, n_row * few)
    scaled_full = jnp.transpose(acts[:, :, :channels], (1, 0, 2)).reshape(tokens, width)
    inputs_full = jnp.transpose(acts[:, :, channels:], (1, 0, 2)).reshape(tokens, width)
    w_out_full = weights[:, :, :hidden].reshape(width, hidden)
    w_in_full = weights[:, :, hidden : 2 * hidden].reshape(width, hidden)

    values = inputs_full.astype(jnp.float32)
    mean = jnp.mean(values, axis=1, keepdims=True)
    centred = values - mean
    rstd = lax.rsqrt(jnp.mean(centred * centred, axis=1, keepdims=True) + 1e-06)
    zhat_full = centred * rstd
    normed_full = (zhat_full * norm_gain + norm_bias).astype(jnp.bfloat16)
    zhat_own = lax.dynamic_slice_in_dim(zhat_full, col_rank * channels, channels, 1)
    gain_own = lax.dynamic_slice_in_dim(norm_gain, col_rank * channels, channels, 0)

    grad_act = jnp.dot(scaled_full, w_out_full, preferred_element_type=jnp.float32)
    grad_pre = (grad_act * gelu_slope(hidden_pre.astype(jnp.float32))).astype(jnp.bfloat16)

    block_w = lax.dot_general(
        normed_full, grad_pre, (((0,), (0,)), ((), ())), preferred_element_type=jnp.float32
    ).astype(jnp.bfloat16)
    if DWIN_VIA == "a2a":
        parts_w = lax.all_to_all(
            block_w.reshape(n_row, width // n_row, hidden), ROW, 0, 0, tiled=True
        )
        d_w_in = jnp.sum(parts_w.astype(jnp.float32), axis=0).astype(jnp.bfloat16)
    elif DWIN_VIA == "two_level":
        core = lax.axis_index("core")
        halves = block_w.reshape(width, 2, hidden // 2)
        kept = lax.dynamic_index_in_dim(halves, core, axis=1, keepdims=False)
        given = lax.dynamic_index_in_dim(halves, 1 - core, axis=1, keepdims=False)
        chip_sum = (kept.astype(jnp.float32) + lax.ppermute(given, "core", SWAP).astype(jnp.float32))
        chip_rows = lax.psum_scatter(chip_sum.astype(jnp.bfloat16), "z", scatter_dimension=0, tiled=True)
        chip_rows = chip_rows.reshape(2, width // n_row, hidden // 2)
        own = lax.dynamic_index_in_dim(chip_rows, core, axis=0, keepdims=False)
        other = lax.ppermute(
            lax.dynamic_index_in_dim(chip_rows, 1 - core, axis=0, keepdims=False), "core", SWAP
        )
        d_w_in = jnp.where(
            core == 0, jnp.concatenate([own, other], axis=1), jnp.concatenate([other, own], axis=1)
        )
    else:
        d_w_in = lax.psum_scatter(block_w, ROW, scatter_dimension=0, tiled=True)

    block_n = lax.dot_general(
        grad_pre, w_in_full, (((1,), (1,)), ((), ())), preferred_element_type=jnp.float32
    ).astype(jnp.bfloat16)
    weighted = block_n.astype(jnp.float32) * norm_gain
    first_part = jnp.sum(weighted, axis=1)
    second_part = jnp.sum(weighted * zhat_full, axis=1)
    f_hi, f_lo = split_hi_lo(first_part)
    s_hi, s_lo = split_hi_lo(second_part)
    sums = jnp.stack([f_hi, f_lo, s_hi, s_lo], axis=1)
    outgoing = jnp.concatenate(
        [
            jnp.transpose(block_n.reshape(tokens, n_col, channels), (1, 0, 2)),
            jnp.broadcast_to(sums[None], (n_col, tokens, 4)),
        ],
        axis=2,
    )
    incoming = lax.all_to_all(outgoing, "col", 0, 0, tiled=True).astype(jnp.float32)
    grad_norm = jnp.sum(incoming[:, :, :channels], axis=0)
    totals = jnp.sum(incoming[:, :, channels:], axis=0)
    first = (totals[:, 0] + totals[:, 1])[:, None] / width
    second = (totals[:, 2] + totals[:, 3])[:, None] / width
    dzhat = grad_norm * gain_own
    grad_conv = (rstd * (dzhat - first - zhat_own * second)).astype(jnp.bfloat16)
    gain_part = jnp.sum(grad_norm * zhat_own, axis=0)
    bias_part = jnp.sum(grad_norm, axis=0)

    per_image = H // rows
    grid = grad_conv.reshape(rows, H, channels)
    down_pairs = [(i, i + 1) for i in range(n_row) if (i + 1) % per_image != 0]
    up_pairs = [(i + 1, i) for i in range(n_row) if (i + 1) % per_image != 0]
    from_above = lax.ppermute(grid[rows - HALO :], ROW, down_pairs)
    from_below = lax.ppermute(grid[:HALO], ROW, up_pairs)
    tall = jnp.concatenate([from_above, grid, from_below], axis=0)
    padded = jnp.pad(tall, ((0, 0), (HALO, HALO), (0, 0)))
    d_input, kernel_sums = conv_call(
        padded,
        block_input.reshape(rows, H, channels),
        cotangent.reshape(rows, H, channels),
        kernel_rows_full,
    )
    d_input = d_input.reshape(tokens, channels)

    kernel_part = kernel_sums.reshape(KS * KS, n_row, few)
    kernel_part = jnp.transpose(kernel_part, (1, 0, 2)).reshape(n_row, KS * KS * few)
    norm_part = jnp.broadcast_to(jnp.concatenate([gain_part, bias_part])[None], (n_row, 2 * channels))
    reduced = jnp.sum(
        lax.all_to_all(jnp.concatenate([kernel_part, norm_part], axis=1), ROW, 0, 0, tiled=True),
        axis=0,
    )
    d_kernel = reduced[: KS * KS * few].reshape(KS * KS, few)
    d_gain = reduced[KS * KS * few : KS * KS * few + channels]
    d_bias = reduced[KS * KS * few + channels :]
    return (d_input, d_kernel, d_gain, d_bias, d_w_in)


def solution(mesh):
    devices = mesh.devices
    split = Mesh(devices.reshape(devices.shape[0] // 2, 2, devices.shape[1]), ROW + ("col",))
    return jax.shard_map(
        body,
        mesh=split,
        in_specs=(
            P(ROW, "col"),
            P(ROW, "col"),
            P(ROW, "col"),
            P(ROW, "col"),
            P(None, ("col",) + ROW),
            P(),
            P(),
            P("col"),
            P(ROW, "col"),
            P(ROW, "col"),
        ),
        out_specs=(P(ROW, "col"), P(None, ("col",) + ROW), P("col"), P("col"), P(ROW, "col")),
        check_vma=False,
    )
```

```python
import jax
import jax.numpy as jnp
from jax import lax
from jax.experimental import pallas as pl
from jax.experimental.pallas import tpu as pltpu
from jax.sharding import Mesh, PartitionSpec as P

KS = 7
H = 64
HALO = KS // 2

WEIGHTS_VIA = "gather"
ROW = ("z", "core")
SWAP = [(0, 1), (1, 0)]
ACTS_VIA = "a2a"


def gelu_slope(values):
    cdf = 0.5 * (1.0 + lax.erf(values * 0.7071067811865476))
    density = jnp.exp(-0.5 * values * values) * 0.3989422804014327
    return cdf + values * density


def gather_blocks(x, axis_name, size, via):
    if via == "a2a":
        wide = jnp.broadcast_to(x[None], (size,) + x.shape)
        return lax.all_to_all(wide, axis_name, 0, 0, tiled=True)
    return lax.all_gather(x, axis_name, axis=0, tiled=False)


def split_three(values):
    high = lax.reduce_precision(values, exponent_bits=8, mantissa_bits=7)
    rest = values - high
    middle = lax.reduce_precision(rest, exponent_bits=8, mantissa_bits=7)
    low = rest - middle
    return jnp.stack([high, middle, low]).astype(jnp.bfloat16)


def conv_body(tall_ref, inputs_ref, cot_ref, kernel_ref, din_ref, dk_ref, pad_ref):
    rows, span, channels = inputs_ref.shape
    pad_ref[...] = tall_ref[...].astype(jnp.float32)
    inputs = inputs_ref[...].astype(jnp.float32)
    moved = jnp.zeros((rows, span, channels), jnp.float32)
    for down in range(KS):
        for across in range(KS):
            tap = down * KS + across
            window = pad_ref[
                2 * HALO - down : 2 * HALO - down + rows,
                2 * HALO - across : 2 * HALO - across + span,
                :,
            ]
            moved = moved + kernel_ref[tap : tap + 1, :][None] * window
            dk_ref[tap : tap + 1, :] = jnp.sum(window * inputs, axis=(0, 1))[None]
    din_ref[...] = (moved + cot_ref[...].astype(jnp.float32)).astype(din_ref.dtype)


def conv_call(padded, inputs, cot, kernel_full):
    rows, span, channels = inputs.shape
    return pl.pallas_call(
        conv_body,
        out_shape=(
            jax.ShapeDtypeStruct((rows, span, channels), jnp.bfloat16),
            jax.ShapeDtypeStruct((KS * KS, channels), jnp.float32),
        ),
        scratch_shapes=[pltpu.VMEM(padded.shape, jnp.float32)],
    )(padded, inputs, cot, kernel_full)


def split_hi_lo(values):
    high = lax.reduce_precision(values, exponent_bits=8, mantissa_bits=7)
    low = values - high
    return high.astype(jnp.bfloat16), low.astype(jnp.bfloat16)


def body(
    block_input,
    conv_out,
    hidden_pre,
    cotangent,
    conv_kernel,
    norm_gain,
    norm_bias,
    layer_scale,
    w_in,
    w_out,
):
    tokens, channels = block_input.shape
    width = norm_gain.shape[0]
    hidden = hidden_pre.shape[1]
    n_col = width // channels
    n_row = width // w_in.shape[0]
    few = conv_kernel.shape[1]
    rows = tokens // H
    col_rank = lax.axis_index("col")
    row_rank = lax.axis_index(ROW)

    scaled = (cotangent.astype(jnp.float32) * layer_scale).astype(jnp.bfloat16)
    acts = gather_blocks(jnp.concatenate([scaled, conv_out], axis=1), "col", n_col, ACTS_VIA)
    kernel_bits = split_three(conv_kernel).reshape(-1)
    lanes_extra = -(-kernel_bits.shape[0] // w_in.shape[0])
    kernel_bits = jnp.pad(kernel_bits, (0, lanes_extra * w_in.shape[0] - kernel_bits.shape[0]))
    weights = gather_blocks(
        jnp.concatenate([w_out, w_in, kernel_bits.reshape(w_in.shape[0], lanes_extra)], axis=1),
        ROW,
        n_row,
        WEIGHTS_VIA,
    )
    kernel_parts = weights[:, :, 2 * hidden :].reshape(n_row, -1)[:, : 3 * KS * KS * few]
    kernel_parts = kernel_parts.reshape(n_row, 3, KS * KS, few).astype(jnp.float32)
    kernel_sum = kernel_parts[:, 0] + kernel_parts[:, 1] + kernel_parts[:, 2]
    kernel_rows_full = jnp.transpose(kernel_sum, (1, 0, 2)).reshape(KS * KS, n_row * few)
    scaled_full = jnp.transpose(acts[:, :, :channels], (1, 0, 2)).reshape(tokens, width)
    inputs_full = jnp.transpose(acts[:, :, channels:], (1, 0, 2)).reshape(tokens, width)
    w_out_full = weights[:, :, :hidden].reshape(width, hidden)
    w_in_full = weights[:, :, hidden : 2 * hidden].reshape(width, hidden)

    values = inputs_full.astype(jnp.float32)
    mean = jnp.mean(values, axis=1, keepdims=True)
    centred = values - mean
    rstd = lax.rsqrt(jnp.mean(centred * centred, axis=1, keepdims=True) + 1e-06)
    zhat_full = centred * rstd
    normed_full = (zhat_full * norm_gain + norm_bias).astype(jnp.bfloat16)
    zhat_own = lax.dynamic_slice_in_dim(zhat_full, col_rank * channels, channels, 1)
    gain_own = lax.dynamic_slice_in_dim(norm_gain, col_rank * channels, channels, 0)

    grad_act = jnp.dot(scaled_full, w_out_full, preferred_element_type=jnp.float32)
    grad_pre = (grad_act * gelu_slope(hidden_pre.astype(jnp.float32))).astype(jnp.bfloat16)

    core = lax.axis_index("core")
    normed_pair = jnp.concatenate([normed_full, lax.ppermute(normed_full, "core", SWAP)], axis=0)
    grad_halves = grad_pre.reshape(tokens, 2, hidden // 2)
    kept = lax.dynamic_index_in_dim(grad_halves, core, axis=1, keepdims=False)
    given = lax.dynamic_index_in_dim(grad_halves, 1 - core, axis=1, keepdims=False)
    grad_pair = jnp.concatenate([kept, lax.ppermute(given, "core", SWAP)], axis=0)
    chip_sum = lax.dot_general(
        normed_pair, grad_pair, (((0,), (0,)), ((), ())), preferred_element_type=jnp.float32
    )
    chip_rows = lax.psum_scatter(chip_sum.astype(jnp.bfloat16), "z", scatter_dimension=0, tiled=True)
    chip_rows = chip_rows.reshape(2, width // n_row, hidden // 2)
    own = lax.dynamic_index_in_dim(chip_rows, core, axis=0, keepdims=False)
    other = lax.ppermute(
        lax.dynamic_index_in_dim(chip_rows, 1 - core, axis=0, keepdims=False), "core", SWAP
    )
    d_w_in = jnp.where(
        core == 0, jnp.concatenate([own, other], axis=1), jnp.concatenate([other, own], axis=1)
    )

    block_n = lax.dot_general(
        grad_pre, w_in_full, (((1,), (1,)), ((), ())), preferred_element_type=jnp.float32
    ).astype(jnp.bfloat16)
    weighted = block_n.astype(jnp.float32) * norm_gain
    first_part = jnp.sum(weighted, axis=1)
    second_part = jnp.sum(weighted * zhat_full, axis=1)
    f_hi, f_lo = split_hi_lo(first_part)
    s_hi, s_lo = split_hi_lo(second_part)
    sums = jnp.stack([f_hi, f_lo, s_hi, s_lo], axis=1)
    outgoing = jnp.concatenate(
        [
            jnp.transpose(block_n.reshape(tokens, n_col, channels), (1, 0, 2)),
            jnp.broadcast_to(sums[None], (n_col, tokens, 4)),
        ],
        axis=2,
    )
    incoming = lax.all_to_all(outgoing, "col", 0, 0, tiled=True).astype(jnp.float32)
    grad_norm = jnp.sum(incoming[:, :, :channels], axis=0)
    totals = jnp.sum(incoming[:, :, channels:], axis=0)
    first = (totals[:, 0] + totals[:, 1])[:, None] / width
    second = (totals[:, 2] + totals[:, 3])[:, None] / width
    dzhat = grad_norm * gain_own
    grad_conv = (rstd * (dzhat - first - zhat_own * second)).astype(jnp.bfloat16)
    gain_part = jnp.sum(grad_norm * zhat_own, axis=0)
    bias_part = jnp.sum(grad_norm, axis=0)

    per_image = H // rows
    grid = grad_conv.reshape(rows, H, channels)
    down_pairs = [(i, i + 1) for i in range(n_row) if (i + 1) % per_image != 0]
    up_pairs = [(i + 1, i) for i in range(n_row) if (i + 1) % per_image != 0]
    from_above = lax.ppermute(grid[rows - HALO :], ROW, down_pairs)
    from_below = lax.ppermute(grid[:HALO], ROW, up_pairs)
    tall = jnp.concatenate([from_above, grid, from_below], axis=0)
    padded = jnp.pad(tall, ((0, 0), (HALO, HALO), (0, 0)))
    d_input, kernel_sums = conv_call(
        padded,
        block_input.reshape(rows, H, channels),
        cotangent.reshape(rows, H, channels),
        kernel_rows_full,
    )
    d_input = d_input.reshape(tokens, channels)

    kernel_part = kernel_sums.reshape(KS * KS, n_row, few)
    kernel_part = jnp.transpose(kernel_part, (1, 0, 2)).reshape(n_row, KS * KS * few)
    norm_part = jnp.broadcast_to(jnp.concatenate([gain_part, bias_part])[None], (n_row, 2 * channels))
    reduced = jnp.sum(
        lax.all_to_all(jnp.concatenate([kernel_part, norm_part], axis=1), ROW, 0, 0, tiled=True),
        axis=0,
    )
    d_kernel = reduced[: KS * KS * few].reshape(KS * KS, few)
    d_gain = reduced[KS * KS * few : KS * KS * few + channels]
    d_bias = reduced[KS * KS * few + channels :]
    return (d_input, d_kernel, d_gain, d_bias, d_w_in)


def solution(mesh):
    devices = mesh.devices
    split = Mesh(devices.reshape(devices.shape[0] // 2, 2, devices.shape[1]), ROW + ("col",))
    return jax.shard_map(
        body,
        mesh=split,
        in_specs=(
            P(ROW, "col"),
            P(ROW, "col"),
            P(ROW, "col"),
            P(ROW, "col"),
            P(None, ("col",) + ROW),
            P(),
            P(),
            P("col"),
            P(ROW, "col"),
            P(ROW, "col"),
        ),
        out_specs=(P(ROW, "col"), P(None, ("col",) + ROW), P("col"), P("col"), P(ROW, "col")),
        check_vma=False,
    )
```

```python
import jax
import jax.numpy as jnp
from jax import lax
from jax.experimental import pallas as pl
from jax.experimental.pallas import tpu as pltpu
from jax.sharding import Mesh, PartitionSpec as P

KS = 7
H = 64
HALO = KS // 2

WEIGHTS_VIA = "gather"
ROW = ("z", "core")
SWAP = [(0, 1), (1, 0)]
ACTS_VIA = "a2a"


def gelu_slope(values):
    cdf = 0.5 * (1.0 + lax.erf(values * 0.7071067811865476))
    density = jnp.exp(-0.5 * values * values) * 0.3989422804014327
    return cdf + values * density


def gather_blocks(x, axis_name, size, via):
    if via == "a2a":
        wide = jnp.broadcast_to(x[None], (size,) + x.shape)
        return lax.all_to_all(wide, axis_name, 0, 0, tiled=True)
    return lax.all_gather(x, axis_name, axis=0, tiled=False)


def split_three(values):
    high = lax.reduce_precision(values, exponent_bits=8, mantissa_bits=7)
    rest = values - high
    middle = lax.reduce_precision(rest, exponent_bits=8, mantissa_bits=7)
    low = rest - middle
    return jnp.stack([high, middle, low]).astype(jnp.bfloat16)


def conv_body(tall_ref, inputs_ref, cot_ref, kernel_ref, din_ref, dk_ref, pad_ref):
    rows, span, channels = inputs_ref.shape
    pad_ref[...] = tall_ref[...].astype(jnp.float32)
    inputs = inputs_ref[...].astype(jnp.float32)
    moved = jnp.zeros((rows, span, channels), jnp.float32)
    for across in range(KS):
        slab = pad_ref[:, 2 * HALO - across : 2 * HALO - across + span, :]
        for down in range(KS):
            tap = down * KS + across
            window = slab[2 * HALO - down : 2 * HALO - down + rows]
            moved = moved + kernel_ref[tap : tap + 1, :][None] * window
            part = jnp.sum(window * inputs, axis=0).reshape(span // 8, 8, channels)
            dk_ref[tap] = jnp.sum(part, axis=0)
    din_ref[...] = (moved + cot_ref[...].astype(jnp.float32)).astype(din_ref.dtype)


def conv_call(padded, inputs, cot, kernel_full):
    rows, span, channels = inputs.shape
    din, dk = pl.pallas_call(
        conv_body,
        out_shape=(
            jax.ShapeDtypeStruct((rows, span, channels), jnp.bfloat16),
            jax.ShapeDtypeStruct((KS * KS, 8, channels), jnp.float32),
        ),
        scratch_shapes=[pltpu.VMEM(padded.shape, jnp.float32)],
    )(padded, inputs, cot, kernel_full)
    return din, jnp.sum(dk, axis=1)


def split_hi_lo(values):
    high = lax.reduce_precision(values, exponent_bits=8, mantissa_bits=7)
    low = values - high
    return high.astype(jnp.bfloat16), low.astype(jnp.bfloat16)


def body(
    block_input,
    conv_out,
    hidden_pre,
    cotangent,
    conv_kernel,
    norm_gain,
    norm_bias,
    layer_scale,
    w_in,
    w_out,
):
    tokens, channels = block_input.shape
    width = norm_gain.shape[0]
    hidden = hidden_pre.shape[1]
    n_col = width // channels
    n_row = width // w_in.shape[0]
    few = conv_kernel.shape[1]
    rows = tokens // H
    col_rank = lax.axis_index("col")
    row_rank = lax.axis_index(ROW)

    scaled = (cotangent.astype(jnp.float32) * layer_scale).astype(jnp.bfloat16)
    acts = gather_blocks(jnp.concatenate([scaled, conv_out], axis=1), "col", n_col, ACTS_VIA)
    kernel_bits = split_three(conv_kernel).reshape(-1)
    lanes_extra = -(-kernel_bits.shape[0] // w_in.shape[0])
    kernel_bits = jnp.pad(kernel_bits, (0, lanes_extra * w_in.shape[0] - kernel_bits.shape[0]))
    weights = gather_blocks(
        jnp.concatenate([w_out, w_in, kernel_bits.reshape(w_in.shape[0], lanes_extra)], axis=1),
        ROW,
        n_row,
        WEIGHTS_VIA,
    )
    kernel_parts = weights[:, :, 2 * hidden :].reshape(n_row, -1)[:, : 3 * KS * KS * few]
    kernel_parts = kernel_parts.reshape(n_row, 3, KS * KS, few).astype(jnp.float32)
    kernel_sum = kernel_parts[:, 0] + kernel_parts[:, 1] + kernel_parts[:, 2]
    kernel_rows_full = jnp.transpose(kernel_sum, (1, 0, 2)).reshape(KS * KS, n_row * few)
    scaled_full = jnp.transpose(acts[:, :, :channels], (1, 0, 2)).reshape(tokens, width)
    inputs_full = jnp.transpose(acts[:, :, channels:], (1, 0, 2)).reshape(tokens, width)
    w_out_full = weights[:, :, :hidden].reshape(width, hidden)
    w_in_full = weights[:, :, hidden : 2 * hidden].reshape(width, hidden)

    values = inputs_full.astype(jnp.float32)
    mean = jnp.mean(values, axis=1, keepdims=True)
    centred = values - mean
    rstd = lax.rsqrt(jnp.mean(centred * centred, axis=1, keepdims=True) + 1e-06)
    zhat_full = centred * rstd
    normed_full = (zhat_full * norm_gain + norm_bias).astype(jnp.bfloat16)
    zhat_own = lax.dynamic_slice_in_dim(zhat_full, col_rank * channels, channels, 1)
    gain_own = lax.dynamic_slice_in_dim(norm_gain, col_rank * channels, channels, 0)

    grad_act = jnp.dot(scaled_full, w_out_full, preferred_element_type=jnp.float32)
    grad_pre = (grad_act * gelu_slope(hidden_pre.astype(jnp.float32))).astype(jnp.bfloat16)

    core = lax.axis_index("core")
    normed_pair = jnp.concatenate([normed_full, lax.ppermute(normed_full, "core", SWAP)], axis=0)
    grad_halves = grad_pre.reshape(tokens, 2, hidden // 2)
    kept = lax.dynamic_index_in_dim(grad_halves, core, axis=1, keepdims=False)
    given = lax.dynamic_index_in_dim(grad_halves, 1 - core, axis=1, keepdims=False)
    grad_pair = jnp.concatenate([kept, lax.ppermute(given, "core", SWAP)], axis=0)
    chip_sum = lax.dot_general(
        normed_pair, grad_pair, (((0,), (0,)), ((), ())), preferred_element_type=jnp.float32
    )
    chip_ready = chip_sum.astype(jnp.bfloat16)
    chip_rows = lax.psum_scatter(chip_ready, "z", scatter_dimension=0, tiled=True)
    chip_rows = chip_rows.reshape(2, width // n_row, hidden // 2)
    own = lax.dynamic_index_in_dim(chip_rows, core, axis=0, keepdims=False)
    other = lax.ppermute(
        lax.dynamic_index_in_dim(chip_rows, 1 - core, axis=0, keepdims=False), "core", SWAP
    )
    d_w_in = jnp.where(
        core == 0, jnp.concatenate([own, other], axis=1), jnp.concatenate([other, own], axis=1)
    )

    block_n = lax.dot_general(
        grad_pre, w_in_full, (((1,), (1,)), ((), ())), preferred_element_type=jnp.float32
    ).astype(jnp.bfloat16)
    weighted = block_n.astype(jnp.float32) * norm_gain
    first_part = jnp.sum(weighted, axis=1)
    second_part = jnp.sum(weighted * zhat_full, axis=1)
    f_hi, f_lo = split_hi_lo(first_part)
    s_hi, s_lo = split_hi_lo(second_part)
    sums = jnp.stack([f_hi, f_lo, s_hi, s_lo], axis=1)
    outgoing = jnp.concatenate(
        [
            jnp.transpose(block_n.reshape(tokens, n_col, channels), (1, 0, 2)),
            jnp.broadcast_to(sums[None], (n_col, tokens, 4)),
        ],
        axis=2,
    )
    chip_ready, outgoing = lax.optimization_barrier((chip_ready, outgoing))
    incoming = lax.all_to_all(outgoing, "col", 0, 0, tiled=True).astype(jnp.float32)
    grad_norm = jnp.sum(incoming[:, :, :channels], axis=0)
    totals = jnp.sum(incoming[:, :, channels:], axis=0)
    first = (totals[:, 0] + totals[:, 1])[:, None] / width
    second = (totals[:, 2] + totals[:, 3])[:, None] / width
    dzhat = grad_norm * gain_own
    grad_conv = (rstd * (dzhat - first - zhat_own * second)).astype(jnp.bfloat16)
    gain_part = jnp.sum(grad_norm * zhat_own, axis=0)
    bias_part = jnp.sum(grad_norm, axis=0)

    per_image = H // rows
    grid = grad_conv.reshape(rows, H, channels)
    down_pairs = [(i, i + 1) for i in range(n_row) if (i + 1) % per_image != 0]
    up_pairs = [(i + 1, i) for i in range(n_row) if (i + 1) % per_image != 0]
    from_above = lax.ppermute(grid[rows - HALO :], ROW, down_pairs)
    from_below = lax.ppermute(grid[:HALO], ROW, up_pairs)
    tall = jnp.concatenate([from_above, grid, from_below], axis=0)
    padded = jnp.pad(tall, ((0, 0), (HALO, HALO), (0, 0)))
    d_input, kernel_sums = conv_call(
        padded,
        block_input.reshape(rows, H, channels),
        cotangent.reshape(rows, H, channels),
        kernel_rows_full,
    )
    d_input = d_input.reshape(tokens, channels)

    kernel_part = kernel_sums.reshape(KS * KS, n_row, few)
    kernel_part = jnp.transpose(kernel_part, (1, 0, 2)).reshape(n_row, KS * KS * few)
    norm_part = jnp.broadcast_to(jnp.concatenate([gain_part, bias_part])[None], (n_row, 2 * channels))
    reduced = jnp.sum(
        lax.all_to_all(jnp.concatenate([kernel_part, norm_part], axis=1), ROW, 0, 0, tiled=True),
        axis=0,
    )
    d_kernel = reduced[: KS * KS * few].reshape(KS * KS, few)
    d_gain = reduced[KS * KS * few : KS * KS * few + channels]
    d_bias = reduced[KS * KS * few + channels :]
    return (d_input, d_kernel, d_gain, d_bias, d_w_in)


def solution(mesh):
    devices = mesh.devices
    split = Mesh(devices.reshape(devices.shape[0] // 2, 2, devices.shape[1]), ROW + ("col",))
    return jax.shard_map(
        body,
        mesh=split,
        in_specs=(
            P(ROW, "col"),
            P(ROW, "col"),
            P(ROW, "col"),
            P(ROW, "col"),
            P(None, ("col",) + ROW),
            P(),
            P(),
            P("col"),
            P(ROW, "col"),
            P(ROW, "col"),
        ),
        out_specs=(P(ROW, "col"), P(None, ("col",) + ROW), P("col"), P("col"), P(ROW, "col")),
        check_vma=False,
    )
```

```python
import jax
import jax.numpy as jnp
from jax import lax
from jax.experimental import pallas as pl
from jax.experimental.pallas import tpu as pltpu
from jax.sharding import Mesh, PartitionSpec as P

KS = 7
H = 64
HALO = KS // 2

WEIGHTS_VIA = "gather"
ROW = ("z", "core")
SWAP = [(0, 1), (1, 0)]
ACTS_VIA = "a2a"


def gelu_slope(values):
    cdf = 0.5 * (1.0 + lax.erf(values * 0.7071067811865476))
    density = jnp.exp(-0.5 * values * values) * 0.3989422804014327
    return cdf + values * density


def gather_blocks(x, axis_name, size, via):
    if via == "a2a":
        wide = jnp.broadcast_to(x[None], (size,) + x.shape)
        return lax.all_to_all(wide, axis_name, 0, 0, tiled=True)
    return lax.all_gather(x, axis_name, axis=0, tiled=False)


def split_three(values):
    high = lax.reduce_precision(values, exponent_bits=8, mantissa_bits=7)
    rest = values - high
    middle = lax.reduce_precision(rest, exponent_bits=8, mantissa_bits=7)
    low = rest - middle
    return jnp.stack([high, middle, low]).astype(jnp.bfloat16)


def conv_body(tall_ref, inputs_ref, cot_ref, kernel_ref, din_ref, dk_ref, pad_ref):
    rows, span, channels = inputs_ref.shape
    pad_ref[...] = tall_ref[...].astype(jnp.float32)
    inputs = inputs_ref[...].astype(jnp.float32)
    moved = jnp.zeros((rows, span, channels), jnp.float32)
    for across in range(KS):
        slab = pad_ref[:, 2 * HALO - across : 2 * HALO - across + span, :]
        for down in range(KS):
            tap = down * KS + across
            window = slab[2 * HALO - down : 2 * HALO - down + rows]
            moved = moved + kernel_ref[tap : tap + 1, :][None] * window
            part = jnp.sum(window * inputs, axis=0).reshape(span // 8, 8, channels)
            dk_ref[tap] = jnp.sum(part, axis=0)
    din_ref[...] = (moved + cot_ref[...].astype(jnp.float32)).astype(din_ref.dtype)


def conv_call(padded, inputs, cot, kernel_full):
    rows, span, channels = inputs.shape
    din, dk = pl.pallas_call(
        conv_body,
        out_shape=(
            jax.ShapeDtypeStruct((rows, span, channels), jnp.bfloat16),
            jax.ShapeDtypeStruct((KS * KS, 8, channels), jnp.float32),
        ),
        scratch_shapes=[pltpu.VMEM(padded.shape, jnp.float32)],
    )(padded, inputs, cot, kernel_full)
    return din, jnp.sum(dk, axis=1)


def split_hi_lo(values):
    high = lax.reduce_precision(values, exponent_bits=8, mantissa_bits=7)
    low = values - high
    return high.astype(jnp.bfloat16), low.astype(jnp.bfloat16)


def body(
    block_input,
    conv_out,
    hidden_pre,
    cotangent,
    conv_kernel,
    norm_gain,
    norm_bias,
    layer_scale,
    w_in,
    w_out,
):
    tokens, channels = block_input.shape
    width = norm_gain.shape[0]
    hidden = hidden_pre.shape[1]
    n_col = width // channels
    n_row = width // w_in.shape[0]
    few = conv_kernel.shape[1]
    rows = tokens // H
    col_rank = lax.axis_index("col")
    row_rank = lax.axis_index(ROW)

    scaled = (cotangent.astype(jnp.float32) * layer_scale).astype(jnp.bfloat16)
    acts = gather_blocks(jnp.concatenate([scaled, conv_out], axis=1), "col", n_col, ACTS_VIA)
    kernel_bits = split_three(conv_kernel).reshape(-1)
    lanes_extra = -(-kernel_bits.shape[0] // w_in.shape[0])
    kernel_bits = jnp.pad(kernel_bits, (0, lanes_extra * w_in.shape[0] - kernel_bits.shape[0]))
    weights = gather_blocks(
        jnp.concatenate([w_out, w_in, kernel_bits.reshape(w_in.shape[0], lanes_extra)], axis=1),
        ROW,
        n_row,
        WEIGHTS_VIA,
    )
    kernel_parts = weights[:, :, 2 * hidden :].reshape(n_row, -1)[:, : 3 * KS * KS * few]
    kernel_parts = kernel_parts.reshape(n_row, 3, KS * KS, few).astype(jnp.float32)
    kernel_sum = kernel_parts[:, 0] + kernel_parts[:, 1] + kernel_parts[:, 2]
    kernel_rows_full = jnp.transpose(kernel_sum, (1, 0, 2)).reshape(KS * KS, n_row * few)
    scaled_full = jnp.transpose(acts[:, :, :channels], (1, 0, 2)).reshape(tokens, width)
    inputs_full = jnp.transpose(acts[:, :, channels:], (1, 0, 2)).reshape(tokens, width)
    w_out_full = weights[:, :, :hidden].reshape(width, hidden)
    w_in_full = weights[:, :, hidden : 2 * hidden].reshape(width, hidden)

    values = inputs_full.astype(jnp.float32)
    mean = jnp.mean(values, axis=1, keepdims=True)
    centred = values - mean
    rstd = lax.rsqrt(jnp.mean(centred * centred, axis=1, keepdims=True) + 1e-06)
    zhat_full = centred * rstd
    normed_full = (zhat_full * norm_gain + norm_bias).astype(jnp.bfloat16)
    zhat_own = lax.dynamic_slice_in_dim(zhat_full, col_rank * channels, channels, 1)
    gain_own = lax.dynamic_slice_in_dim(norm_gain, col_rank * channels, channels, 0)

    grad_act = jnp.dot(scaled_full, w_out_full, preferred_element_type=jnp.float32)
    grad_pre = (grad_act * gelu_slope(hidden_pre.astype(jnp.float32))).astype(jnp.bfloat16)

    core = lax.axis_index("core")
    normed_pair = jnp.concatenate([normed_full, lax.ppermute(normed_full, "core", SWAP)], axis=0)
    grad_halves = grad_pre.reshape(tokens, 2, hidden // 2)
    kept = lax.dynamic_index_in_dim(grad_halves, core, axis=1, keepdims=False)
    given = lax.dynamic_index_in_dim(grad_halves, 1 - core, axis=1, keepdims=False)
    grad_pair = jnp.concatenate([kept, lax.ppermute(given, "core", SWAP)], axis=0)
    chip_sum = lax.dot_general(
        normed_pair, grad_pair, (((0,), (0,)), ((), ())), preferred_element_type=jnp.float32
    )
    chip_ready = chip_sum.astype(jnp.bfloat16)
    chip_rows = lax.psum_scatter(chip_ready, "z", scatter_dimension=0, tiled=True)
    chip_rows = chip_rows.reshape(2, width // n_row, hidden // 2)
    own = lax.dynamic_index_in_dim(chip_rows, core, axis=0, keepdims=False)
    other = lax.ppermute(
        lax.dynamic_index_in_dim(chip_rows, 1 - core, axis=0, keepdims=False), "core", SWAP
    )
    d_w_in = jnp.where(
        core == 0, jnp.concatenate([own, other], axis=1), jnp.concatenate([other, own], axis=1)
    )

    block_n = lax.dot_general(
        grad_pre, w_in_full, (((1,), (1,)), ((), ())), preferred_element_type=jnp.float32
    ).astype(jnp.bfloat16)
    weighted = block_n.astype(jnp.float32) * norm_gain
    first_part = jnp.sum(weighted, axis=1)
    second_part = jnp.sum(weighted * zhat_full, axis=1)
    f_hi, f_lo = split_hi_lo(first_part)
    s_hi, s_lo = split_hi_lo(second_part)
    sums = jnp.stack([f_hi, f_lo, s_hi, s_lo], axis=1)
    outgoing = jnp.concatenate(
        [
            jnp.transpose(block_n.reshape(tokens, n_col, channels), (1, 0, 2)),
            jnp.broadcast_to(sums[None], (n_col, tokens, 4)),
        ],
        axis=2,
    )
    incoming = lax.all_to_all(outgoing, "col", 0, 0, tiled=True).astype(jnp.float32)
    grad_norm = jnp.sum(incoming[:, :, :channels], axis=0)
    totals = jnp.sum(incoming[:, :, channels:], axis=0)
    first = (totals[:, 0] + totals[:, 1])[:, None] / width
    second = (totals[:, 2] + totals[:, 3])[:, None] / width
    dzhat = grad_norm * gain_own
    grad_conv = (rstd * (dzhat - first - zhat_own * second)).astype(jnp.bfloat16)
    gain_part = jnp.sum(grad_norm * zhat_own, axis=0)
    bias_part = jnp.sum(grad_norm, axis=0)

    per_image = H // rows
    grid = grad_conv.reshape(rows, H, channels)
    down_pairs = [(i, i + 1) for i in range(n_row) if (i + 1) % per_image != 0]
    up_pairs = [(i + 1, i) for i in range(n_row) if (i + 1) % per_image != 0]
    from_above = lax.ppermute(grid[rows - HALO :], ROW, down_pairs)
    from_below = lax.ppermute(grid[:HALO], ROW, up_pairs)
    tall = jnp.concatenate([from_above, grid, from_below], axis=0)
    padded = jnp.pad(tall, ((0, 0), (HALO, HALO), (0, 0)))
    d_input, kernel_sums = conv_call(
        padded,
        block_input.reshape(rows, H, channels),
        cotangent.reshape(rows, H, channels),
        kernel_rows_full,
    )
    d_input = d_input.reshape(tokens, channels)

    n_chip = n_row // 2
    partials = jnp.concatenate([kernel_sums.reshape(-1), gain_part, bias_part])
    partials = partials + lax.ppermute(partials, "core", SWAP)
    kernel_chip = partials[: KS * KS * channels].reshape(KS * KS, n_chip, 2, few)
    kernel_chip = lax.dynamic_index_in_dim(kernel_chip, core, axis=2, keepdims=False)
    kernel_chip = jnp.transpose(kernel_chip, (1, 0, 2)).reshape(n_chip, KS * KS * few)
    norm_chip = jnp.broadcast_to(partials[None, KS * KS * channels :], (n_chip, 2 * channels))
    reduced = jnp.sum(
        lax.all_to_all(jnp.concatenate([kernel_chip, norm_chip], axis=1), "z", 0, 0, tiled=True),
        axis=0,
    )
    d_kernel = reduced[: KS * KS * few].reshape(KS * KS, few)
    d_gain = reduced[KS * KS * few : KS * KS * few + channels]
    d_bias = reduced[KS * KS * few + channels :]
    return (d_input, d_kernel, d_gain, d_bias, d_w_in)


def solution(mesh):
    devices = mesh.devices
    split = Mesh(devices.reshape(devices.shape[0] // 2, 2, devices.shape[1]), ROW + ("col",))
    return jax.shard_map(
        body,
        mesh=split,
        in_specs=(
            P(ROW, "col"),
            P(ROW, "col"),
            P(ROW, "col"),
            P(ROW, "col"),
            P(None, ("col",) + ROW),
            P(),
            P(),
            P("col"),
            P(ROW, "col"),
            P(ROW, "col"),
        ),
        out_specs=(P(ROW, "col"), P(None, ("col",) + ROW), P("col"), P("col"), P(ROW, "col")),
        check_vma=False,
    )
```

```python
import jax
import jax.numpy as jnp
from jax import lax
from jax.experimental import pallas as pl
from jax.experimental.pallas import tpu as pltpu
from jax.sharding import Mesh, PartitionSpec as P

KS = 7
H = 64
HALO = KS // 2

WEIGHTS_VIA = "gather"
ROW = ("z", "core")
SWAP = [(0, 1), (1, 0)]
ACTS_VIA = "a2a"


def gelu_slope(values):
    cdf = 0.5 * (1.0 + lax.erf(values * 0.7071067811865476))
    density = jnp.exp(-0.5 * values * values) * 0.3989422804014327
    return cdf + values * density


def gather_blocks(x, axis_name, size, via):
    if via == "a2a":
        wide = jnp.broadcast_to(x[None], (size,) + x.shape)
        return lax.all_to_all(wide, axis_name, 0, 0, tiled=True)
    return lax.all_gather(x, axis_name, axis=0, tiled=False)


def split_three(values):
    high = lax.reduce_precision(values, exponent_bits=8, mantissa_bits=7)
    rest = values - high
    middle = lax.reduce_precision(rest, exponent_bits=8, mantissa_bits=7)
    low = rest - middle
    return jnp.stack([high, middle, low]).astype(jnp.bfloat16)


def conv_body(tall_ref, inputs_ref, cot_ref, kernel_ref, din_ref, dk_ref, pad_ref):
    rows, span, channels = inputs_ref.shape
    pad_ref[...] = tall_ref[...].astype(jnp.float32)
    inputs = inputs_ref[...].astype(jnp.float32)
    moved = jnp.zeros((rows, span, channels), jnp.float32)
    for across in range(KS):
        slab = pad_ref[:, 2 * HALO - across : 2 * HALO - across + span, :]
        for down in range(KS):
            tap = down * KS + across
            window = slab[2 * HALO - down : 2 * HALO - down + rows]
            moved = moved + kernel_ref[tap : tap + 1, :][None] * window
            part = jnp.sum(window * inputs, axis=0).reshape(span // 8, 8, channels)
            dk_ref[tap] = jnp.sum(part, axis=0)
    din_ref[...] = (moved + cot_ref[...].astype(jnp.float32)).astype(din_ref.dtype)


def conv_call(padded, inputs, cot, kernel_full):
    rows, span, channels = inputs.shape
    din, dk = pl.pallas_call(
        conv_body,
        out_shape=(
            jax.ShapeDtypeStruct((rows, span, channels), jnp.bfloat16),
            jax.ShapeDtypeStruct((KS * KS, 8, channels), jnp.float32),
        ),
        scratch_shapes=[pltpu.VMEM(padded.shape, jnp.float32)],
    )(padded, inputs, cot, kernel_full)
    return din, jnp.sum(dk, axis=1)


def split_hi_lo(values):
    high = lax.reduce_precision(values, exponent_bits=8, mantissa_bits=7)
    low = values - high
    return high.astype(jnp.bfloat16), low.astype(jnp.bfloat16)


def body(
    block_input,
    conv_out,
    hidden_pre,
    cotangent,
    conv_kernel,
    norm_gain,
    norm_bias,
    layer_scale,
    w_in,
    w_out,
):
    tokens, channels = block_input.shape
    width = norm_gain.shape[0]
    hidden = hidden_pre.shape[1]
    n_col = width // channels
    n_row = width // w_in.shape[0]
    few = conv_kernel.shape[1]
    rows = tokens // H
    col_rank = lax.axis_index("col")
    row_rank = lax.axis_index(ROW)

    scaled = (cotangent.astype(jnp.float32) * layer_scale).astype(jnp.bfloat16)
    acts = gather_blocks(jnp.concatenate([scaled, conv_out], axis=1), "col", n_col, ACTS_VIA)
    kernel_bits = split_three(conv_kernel).reshape(-1)
    lanes_extra = -(-kernel_bits.shape[0] // w_in.shape[0])
    kernel_bits = jnp.pad(kernel_bits, (0, lanes_extra * w_in.shape[0] - kernel_bits.shape[0]))
    weights = gather_blocks(
        jnp.concatenate([w_out, w_in, kernel_bits.reshape(w_in.shape[0], lanes_extra)], axis=1),
        ROW,
        n_row,
        WEIGHTS_VIA,
    )
    kernel_parts = weights[:, :, 2 * hidden :].reshape(n_row, -1)[:, : 3 * KS * KS * few]
    kernel_parts = kernel_parts.reshape(n_row, 3, KS * KS, few).astype(jnp.float32)
    kernel_sum = kernel_parts[:, 0] + kernel_parts[:, 1] + kernel_parts[:, 2]
    kernel_rows_full = jnp.transpose(kernel_sum, (1, 0, 2)).reshape(KS * KS, n_row * few)
    scaled_full = jnp.transpose(acts[:, :, :channels], (1, 0, 2)).reshape(tokens, width)
    inputs_full = jnp.transpose(acts[:, :, channels:], (1, 0, 2)).reshape(tokens, width)
    w_out_full = weights[:, :, :hidden].reshape(width, hidden)
    w_in_full = weights[:, :, hidden : 2 * hidden].reshape(width, hidden)

    values = inputs_full.astype(jnp.float32)
    mean = jnp.mean(values, axis=1, keepdims=True)
    centred = values - mean
    rstd = lax.rsqrt(jnp.mean(centred * centred, axis=1, keepdims=True) + 1e-06)
    zhat_full = centred * rstd
    normed_full = (zhat_full * norm_gain + norm_bias).astype(jnp.bfloat16)
    zhat_own = lax.dynamic_slice_in_dim(zhat_full, col_rank * channels, channels, 1)
    gain_own = lax.dynamic_slice_in_dim(norm_gain, col_rank * channels, channels, 0)

    grad_act = jnp.dot(scaled_full, w_out_full, preferred_element_type=jnp.float32)
    grad_pre = (grad_act * gelu_slope(hidden_pre.astype(jnp.float32))).astype(jnp.bfloat16)

    core = lax.axis_index("core")
    normed_pair = jnp.concatenate([normed_full, lax.ppermute(normed_full, "core", SWAP)], axis=0)
    grad_halves = grad_pre.reshape(tokens, 2, hidden // 2)
    kept = lax.dynamic_index_in_dim(grad_halves, core, axis=1, keepdims=False)
    given = lax.dynamic_index_in_dim(grad_halves, 1 - core, axis=1, keepdims=False)
    grad_pair = jnp.concatenate([kept, lax.ppermute(given, "core", SWAP)], axis=0)
    chip_sum = lax.dot_general(
        normed_pair, grad_pair, (((0,), (0,)), ((), ())), preferred_element_type=jnp.float32
    )
    chip_ready = chip_sum.astype(jnp.bfloat16)
    chip_rows = lax.psum_scatter(chip_ready, "z", scatter_dimension=0, tiled=True)
    chip_rows = chip_rows.reshape(2, width // n_row, hidden // 2)
    own = lax.dynamic_index_in_dim(chip_rows, core, axis=0, keepdims=False)
    other = lax.ppermute(
        lax.dynamic_index_in_dim(chip_rows, 1 - core, axis=0, keepdims=False), "core", SWAP
    )
    d_w_in = jnp.where(
        core == 0, jnp.concatenate([own, other], axis=1), jnp.concatenate([other, own], axis=1)
    )

    block_n = lax.dot_general(
        grad_pre, w_in_full, (((1,), (1,)), ((), ())), preferred_element_type=jnp.float32
    ).astype(jnp.bfloat16)
    weighted = block_n.astype(jnp.float32) * norm_gain
    first_part = jnp.sum(weighted, axis=1)
    second_part = jnp.sum(weighted * zhat_full, axis=1)
    f_hi, f_lo = split_hi_lo(first_part)
    s_hi, s_lo = split_hi_lo(second_part)
    sums = jnp.stack([f_hi, f_lo, s_hi, s_lo], axis=1)
    outgoing = jnp.concatenate(
        [
            jnp.transpose(block_n.reshape(tokens, n_col, channels), (1, 0, 2)),
            jnp.broadcast_to(sums[None], (n_col, tokens, 4)),
        ],
        axis=2,
    )
    incoming = lax.all_to_all(outgoing, "col", 0, 0, tiled=True)
    grad_norm = jnp.sum(incoming[:, :, :channels].astype(jnp.float32), axis=0)
    totals = jnp.sum(incoming[:, :, channels:].astype(jnp.float32), axis=0)
    first = (totals[:, 0] + totals[:, 1])[:, None] / width
    second = (totals[:, 2] + totals[:, 3])[:, None] / width
    dzhat = grad_norm * gain_own
    grad_conv = (rstd * (dzhat - first - zhat_own * second)).astype(jnp.bfloat16)
    gain_part = jnp.sum(grad_norm * zhat_own, axis=0)
    bias_part = jnp.sum(grad_norm, axis=0)

    per_image = H // rows
    grid = grad_conv.reshape(rows, H, channels)
    down_pairs = [(i, i + 1) for i in range(n_row) if (i + 1) % per_image != 0]
    up_pairs = [(i + 1, i) for i in range(n_row) if (i + 1) % per_image != 0]
    from_above = lax.ppermute(grid[rows - HALO :], ROW, down_pairs)
    from_below = lax.ppermute(grid[:HALO], ROW, up_pairs)
    tall = jnp.concatenate([from_above, grid, from_below], axis=0)
    padded = jnp.pad(tall, ((0, 0), (HALO, HALO), (0, 0)))
    d_input, kernel_sums = conv_call(
        padded,
        block_input.reshape(rows, H, channels),
        cotangent.reshape(rows, H, channels),
        kernel_rows_full,
    )
    d_input = d_input.reshape(tokens, channels)

    n_chip = n_row // 2
    partials = jnp.concatenate([kernel_sums.reshape(-1), gain_part, bias_part])
    partials = partials + lax.ppermute(partials, "core", SWAP)
    kernel_chip = partials[: KS * KS * channels].reshape(KS * KS, n_chip, 2, few)
    kernel_chip = lax.dynamic_index_in_dim(kernel_chip, core, axis=2, keepdims=False)
    kernel_chip = jnp.transpose(kernel_chip, (1, 0, 2)).reshape(n_chip, KS * KS * few)
    norm_chip = jnp.broadcast_to(partials[None, KS * KS * channels :], (n_chip, 2 * channels))
    reduced = jnp.sum(
        lax.all_to_all(jnp.concatenate([kernel_chip, norm_chip], axis=1), "z", 0, 0, tiled=True),
        axis=0,
    )
    d_kernel = reduced[: KS * KS * few].reshape(KS * KS, few)
    d_gain = reduced[KS * KS * few : KS * KS * few + channels]
    d_bias = reduced[KS * KS * few + channels :]
    return (d_input, d_kernel, d_gain, d_bias, d_w_in)


def solution(mesh):
    devices = mesh.devices
    split = Mesh(devices.reshape(devices.shape[0] // 2, 2, devices.shape[1]), ROW + ("col",))
    return jax.shard_map(
        body,
        mesh=split,
        in_specs=(
            P(ROW, "col"),
            P(ROW, "col"),
            P(ROW, "col"),
            P(ROW, "col"),
            P(None, ("col",) + ROW),
            P(),
            P(),
            P("col"),
            P(ROW, "col"),
            P(ROW, "col"),
        ),
        out_specs=(P(ROW, "col"), P(None, ("col",) + ROW), P("col"), P("col"), P(ROW, "col")),
        check_vma=False,
    )
```

```python
import jax
import jax.numpy as jnp
from jax import lax
from jax.experimental import pallas as pl
from jax.experimental.pallas import tpu as pltpu
from jax.sharding import Mesh, PartitionSpec as P

KS = 7
H = 64
HALO = KS // 2

WEIGHTS_VIA = "gather"
ROW = ("z", "core")
SWAP = [(0, 1), (1, 0)]
ACTS_VIA = "a2a"


def gelu_slope(values):
    cdf = 0.5 * (1.0 + lax.erf(values * 0.7071067811865476))
    density = jnp.exp(-0.5 * values * values) * 0.3989422804014327
    return cdf + values * density


def gather_blocks(x, axis_name, size, via):
    if via == "a2a":
        wide = jnp.broadcast_to(x[None], (size,) + x.shape)
        return lax.all_to_all(wide, axis_name, 0, 0, tiled=True)
    return lax.all_gather(x, axis_name, axis=0, tiled=False)


def split_three(values):
    high = lax.reduce_precision(values, exponent_bits=8, mantissa_bits=7)
    rest = values - high
    middle = lax.reduce_precision(rest, exponent_bits=8, mantissa_bits=7)
    low = rest - middle
    return jnp.stack([high, middle, low]).astype(jnp.bfloat16)


def conv_body(tall_ref, inputs_ref, cot_ref, kernel_ref, din_ref, dk_ref, pad_ref):
    rows, span, channels = inputs_ref.shape
    pad_ref[...] = tall_ref[...].astype(jnp.float32)
    inputs = inputs_ref[...].astype(jnp.float32)
    moved = jnp.zeros((rows, span, channels), jnp.float32)
    for across in range(KS):
        slab = pad_ref[:, 2 * HALO - across : 2 * HALO - across + span, :]
        for down in range(KS):
            tap = down * KS + across
            window = slab[2 * HALO - down : 2 * HALO - down + rows]
            moved = moved + kernel_ref[tap : tap + 1, :][None] * window
            part = jnp.sum(window * inputs, axis=0).reshape(span // 8, 8, channels)
            dk_ref[tap] = jnp.sum(part, axis=0)
    din_ref[...] = (moved + cot_ref[...].astype(jnp.float32)).astype(din_ref.dtype)


def conv_call(padded, inputs, cot, kernel_full):
    rows, span, channels = inputs.shape
    din, dk = pl.pallas_call(
        conv_body,
        out_shape=(
            jax.ShapeDtypeStruct((rows, span, channels), jnp.bfloat16),
            jax.ShapeDtypeStruct((KS * KS, 8, channels), jnp.float32),
        ),
        scratch_shapes=[pltpu.VMEM(padded.shape, jnp.float32)],
    )(padded, inputs, cot, kernel_full)
    return din, jnp.sum(dk, axis=1)


def split_hi_lo(values):
    high = lax.reduce_precision(values, exponent_bits=8, mantissa_bits=7)
    low = values - high
    return high.astype(jnp.bfloat16), low.astype(jnp.bfloat16)


def body(
    block_input,
    conv_out,
    hidden_pre,
    cotangent,
    conv_kernel,
    norm_gain,
    norm_bias,
    layer_scale,
    w_in,
    w_out,
):
    tokens, channels = block_input.shape
    width = norm_gain.shape[0]
    hidden = hidden_pre.shape[1]
    n_col = width // channels
    n_row = width // w_in.shape[0]
    few = conv_kernel.shape[1]
    rows = tokens // H
    col_rank = lax.axis_index("col")
    row_rank = lax.axis_index(ROW)

    scaled = (cotangent.astype(jnp.float32) * layer_scale).astype(jnp.bfloat16)
    acts = gather_blocks(jnp.concatenate([scaled, conv_out], axis=1), "col", n_col, ACTS_VIA)
    kernel_bits = split_three(conv_kernel).reshape(-1)
    lanes_extra = -(-kernel_bits.shape[0] // w_in.shape[0])
    kernel_bits = jnp.pad(kernel_bits, (0, lanes_extra * w_in.shape[0] - kernel_bits.shape[0]))
    weights = gather_blocks(
        jnp.concatenate([w_out, w_in, kernel_bits.reshape(w_in.shape[0], lanes_extra)], axis=1),
        ROW,
        n_row,
        WEIGHTS_VIA,
    )
    kernel_parts = weights[:, :, 2 * hidden :].reshape(n_row, -1)[:, : 3 * KS * KS * few]
    kernel_parts = kernel_parts.reshape(n_row, 3, KS * KS, few).astype(jnp.float32)
    kernel_sum = kernel_parts[:, 0] + kernel_parts[:, 1] + kernel_parts[:, 2]
    kernel_rows_full = jnp.transpose(kernel_sum, (1, 0, 2)).reshape(KS * KS, n_row * few)
    scaled_full = jnp.transpose(acts[:, :, :channels], (1, 0, 2)).reshape(tokens, width)
    inputs_full = jnp.transpose(acts[:, :, channels:], (1, 0, 2)).reshape(tokens, width)
    w_out_full = weights[:, :, :hidden].reshape(width, hidden)
    w_in_full = weights[:, :, hidden : 2 * hidden].reshape(width, hidden)

    values = inputs_full.astype(jnp.float32)
    mean = jnp.mean(values, axis=1, keepdims=True)
    centred = values - mean
    rstd = lax.rsqrt(jnp.mean(centred * centred, axis=1, keepdims=True) + 1e-06)
    zhat_full = centred * rstd
    normed_full = (zhat_full * norm_gain + norm_bias).astype(jnp.bfloat16)
    zhat_own = lax.dynamic_slice_in_dim(zhat_full, col_rank * channels, channels, 1)
    gain_own = lax.dynamic_slice_in_dim(norm_gain, col_rank * channels, channels, 0)

    grad_act = jnp.dot(scaled_full, w_out_full, preferred_element_type=jnp.float32)
    grad_pre = (grad_act * gelu_slope(hidden_pre.astype(jnp.float32))).astype(jnp.bfloat16)

    core = lax.axis_index("core")
    normed_pair = jnp.concatenate([normed_full, lax.ppermute(normed_full, "core", SWAP)], axis=0)
    grad_halves = grad_pre.reshape(tokens, 2, hidden // 2)
    kept = lax.dynamic_index_in_dim(grad_halves, core, axis=1, keepdims=False)
    given = lax.dynamic_index_in_dim(grad_halves, 1 - core, axis=1, keepdims=False)
    grad_pair = jnp.concatenate([kept, lax.ppermute(given, "core", SWAP)], axis=0)
    chip_sum = lax.dot_general(
        normed_pair, grad_pair, (((0,), (0,)), ((), ())), preferred_element_type=jnp.float32
    )
    chip_ready = chip_sum.astype(jnp.bfloat16)
    chip_rows = lax.psum_scatter(chip_ready, "z", scatter_dimension=0, tiled=True)
    chip_rows = chip_rows.reshape(2, width // n_row, hidden // 2)
    own = lax.dynamic_index_in_dim(chip_rows, core, axis=0, keepdims=False)
    other = lax.ppermute(
        lax.dynamic_index_in_dim(chip_rows, 1 - core, axis=0, keepdims=False), "core", SWAP
    )
    d_w_in = jnp.where(
        core == 0, jnp.concatenate([own, other], axis=1), jnp.concatenate([other, own], axis=1)
    )

    block_n = lax.dot_general(
        w_in_full.reshape(n_col, channels, hidden),
        grad_pre,
        (((2,), (1,)), ((), ())),
        preferred_element_type=jnp.float32,
    ).astype(jnp.bfloat16)
    zhat_by_owner = jnp.transpose(zhat_full.reshape(tokens, n_col, channels), (1, 2, 0))
    weighted = block_n.astype(jnp.float32) * norm_gain.reshape(n_col, channels, 1)
    first_part = jnp.sum(weighted, axis=(0, 1))
    second_part = jnp.sum(weighted * zhat_by_owner, axis=(0, 1))
    f_hi, f_lo = split_hi_lo(first_part)
    s_hi, s_lo = split_hi_lo(second_part)
    sums = jnp.stack([f_hi, f_lo, s_hi, s_lo], axis=0)
    outgoing = jnp.concatenate([block_n, jnp.broadcast_to(sums[None], (n_col, 4, tokens))], axis=1)
    incoming = lax.all_to_all(outgoing, "col", 0, 0, tiled=True)
    grad_norm = jnp.sum(incoming[:, :channels].astype(jnp.float32), axis=0).T
    totals = jnp.sum(incoming[:, channels:].astype(jnp.float32), axis=0).T
    first = (totals[:, 0] + totals[:, 1])[:, None] / width
    second = (totals[:, 2] + totals[:, 3])[:, None] / width
    dzhat = grad_norm * gain_own
    grad_conv = (rstd * (dzhat - first - zhat_own * second)).astype(jnp.bfloat16)
    gain_part = jnp.sum(grad_norm * zhat_own, axis=0)
    bias_part = jnp.sum(grad_norm, axis=0)

    per_image = H // rows
    grid = grad_conv.reshape(rows, H, channels)
    down_pairs = [(i, i + 1) for i in range(n_row) if (i + 1) % per_image != 0]
    up_pairs = [(i + 1, i) for i in range(n_row) if (i + 1) % per_image != 0]
    from_above = lax.ppermute(grid[rows - HALO :], ROW, down_pairs)
    from_below = lax.ppermute(grid[:HALO], ROW, up_pairs)
    tall = jnp.concatenate([from_above, grid, from_below], axis=0)
    padded = jnp.pad(tall, ((0, 0), (HALO, HALO), (0, 0)))
    d_input, kernel_sums = conv_call(
        padded,
        block_input.reshape(rows, H, channels),
        cotangent.reshape(rows, H, channels),
        kernel_rows_full,
    )
    d_input = d_input.reshape(tokens, channels)

    n_chip = n_row // 2
    partials = jnp.concatenate([kernel_sums.reshape(-1), gain_part, bias_part])
    partials = partials + lax.ppermute(partials, "core", SWAP)
    kernel_chip = partials[: KS * KS * channels].reshape(KS * KS, n_chip, 2, few)
    kernel_chip = lax.dynamic_index_in_dim(kernel_chip, core, axis=2, keepdims=False)
    kernel_chip = jnp.transpose(kernel_chip, (1, 0, 2)).reshape(n_chip, KS * KS * few)
    norm_chip = jnp.broadcast_to(partials[None, KS * KS * channels :], (n_chip, 2 * channels))
    reduced = jnp.sum(
        lax.all_to_all(jnp.concatenate([kernel_chip, norm_chip], axis=1), "z", 0, 0, tiled=True),
        axis=0,
    )
    d_kernel = reduced[: KS * KS * few].reshape(KS * KS, few)
    d_gain = reduced[KS * KS * few : KS * KS * few + channels]
    d_bias = reduced[KS * KS * few + channels :]
    return (d_input, d_kernel, d_gain, d_bias, d_w_in)


def solution(mesh):
    devices = mesh.devices
    split = Mesh(devices.reshape(devices.shape[0] // 2, 2, devices.shape[1]), ROW + ("col",))
    return jax.shard_map(
        body,
        mesh=split,
        in_specs=(
            P(ROW, "col"),
            P(ROW, "col"),
            P(ROW, "col"),
            P(ROW, "col"),
            P(None, ("col",) + ROW),
            P(),
            P(),
            P("col"),
            P(ROW, "col"),
            P(ROW, "col"),
        ),
        out_specs=(P(ROW, "col"), P(None, ("col",) + ROW), P("col"), P("col"), P(ROW, "col")),
        check_vma=False,
    )
```

```python
import jax
import jax.numpy as jnp
from jax import lax
from jax.experimental import pallas as pl
from jax.experimental.pallas import tpu as pltpu
from jax.sharding import Mesh, PartitionSpec as P

KS = 7
H = 64
HALO = KS // 2

WEIGHTS_VIA = "gather"
ROW = ("z", "core")
SWAP = [(0, 1), (1, 0)]
ACTS_VIA = "a2a"


def gelu_slope(values):
    cdf = 0.5 * (1.0 + lax.erf(values * 0.7071067811865476))
    density = jnp.exp(-0.5 * values * values) * 0.3989422804014327
    return cdf + values * density


def gather_blocks(x, axis_name, size, via):
    if via == "a2a":
        wide = jnp.broadcast_to(x[None], (size,) + x.shape)
        return lax.all_to_all(wide, axis_name, 0, 0, tiled=True)
    return lax.all_gather(x, axis_name, axis=0, tiled=False)


def split_three(values):
    high = lax.reduce_precision(values, exponent_bits=8, mantissa_bits=7)
    rest = values - high
    middle = lax.reduce_precision(rest, exponent_bits=8, mantissa_bits=7)
    low = rest - middle
    return jnp.stack([high, middle, low]).astype(jnp.bfloat16)


def conv_body(tall_ref, inputs_ref, cot_ref, kernel_ref, din_ref, dk_ref, pad_ref):
    rows, span, channels = inputs_ref.shape
    pad_ref[...] = tall_ref[...].astype(jnp.float32)
    inputs = inputs_ref[...].astype(jnp.float32)
    moved = jnp.zeros((rows, span, channels), jnp.float32)
    for across in range(KS):
        slab = pad_ref[:, 2 * HALO - across : 2 * HALO - across + span, :]
        for down in range(KS):
            tap = down * KS + across
            window = slab[2 * HALO - down : 2 * HALO - down + rows]
            moved = moved + kernel_ref[tap : tap + 1, :][None] * window
            part = jnp.sum(window * inputs, axis=0).reshape(span // 8, 8, channels)
            dk_ref[tap] = jnp.sum(part, axis=0)
    din_ref[...] = (moved + cot_ref[...].astype(jnp.float32)).astype(din_ref.dtype)


def conv_call(padded, inputs, cot, kernel_full):
    rows, span, channels = inputs.shape
    din, dk = pl.pallas_call(
        conv_body,
        out_shape=(
            jax.ShapeDtypeStruct((rows, span, channels), jnp.bfloat16),
            jax.ShapeDtypeStruct((KS * KS, 8, channels), jnp.float32),
        ),
        scratch_shapes=[pltpu.VMEM(padded.shape, jnp.float32)],
    )(padded, inputs, cot, kernel_full)
    return din, jnp.sum(dk, axis=1)


def split_hi_lo(values):
    high = lax.reduce_precision(values, exponent_bits=8, mantissa_bits=7)
    low = values - high
    return high.astype(jnp.bfloat16), low.astype(jnp.bfloat16)


def body(
    block_input,
    conv_out,
    hidden_pre,
    cotangent,
    conv_kernel,
    norm_gain,
    norm_bias,
    layer_scale,
    w_in,
    w_out,
):
    tokens, channels = block_input.shape
    width = norm_gain.shape[0]
    hidden = hidden_pre.shape[1]
    n_col = width // channels
    n_row = width // w_in.shape[0]
    few = conv_kernel.shape[1]
    rows = tokens // H
    col_rank = lax.axis_index("col")
    row_rank = lax.axis_index(ROW)

    scaled = (cotangent.astype(jnp.float32) * layer_scale).astype(jnp.bfloat16)
    acts = gather_blocks(jnp.concatenate([scaled, conv_out], axis=1), "col", n_col, ACTS_VIA)
    kernel_bits = split_three(conv_kernel).reshape(-1)
    lanes_extra = -(-kernel_bits.shape[0] // w_in.shape[0])
    kernel_bits = jnp.pad(kernel_bits, (0, lanes_extra * w_in.shape[0] - kernel_bits.shape[0]))
    weights = gather_blocks(
        jnp.concatenate([w_out, w_in, kernel_bits.reshape(w_in.shape[0], lanes_extra)], axis=1),
        ROW,
        n_row,
        WEIGHTS_VIA,
    )
    kernel_parts = weights[:, :, 2 * hidden :].reshape(n_row, -1)[:, : 3 * KS * KS * few]
    kernel_parts = kernel_parts.reshape(n_row, 3, KS * KS, few).astype(jnp.float32)
    kernel_sum = kernel_parts[:, 0] + kernel_parts[:, 1] + kernel_parts[:, 2]
    kernel_rows_full = jnp.transpose(kernel_sum, (1, 0, 2)).reshape(KS * KS, n_row * few)
    scaled_full = jnp.transpose(acts[:, :, :channels], (1, 0, 2)).reshape(tokens, width)
    inputs_full = jnp.transpose(acts[:, :, channels:], (1, 0, 2)).reshape(tokens, width)
    w_out_full = weights[:, :, :hidden].reshape(width, hidden)
    w_in_full = weights[:, :, hidden : 2 * hidden].reshape(width, hidden)

    values = inputs_full.astype(jnp.float32)
    mean = jnp.mean(values, axis=1, keepdims=True)
    centred = values - mean
    rstd = lax.rsqrt(jnp.mean(centred * centred, axis=1, keepdims=True) + 1e-06)
    zhat_full = centred * rstd
    normed_full = (zhat_full * norm_gain + norm_bias).astype(jnp.bfloat16)
    zhat_own = lax.dynamic_slice_in_dim(zhat_full, col_rank * channels, channels, 1)
    gain_own = lax.dynamic_slice_in_dim(norm_gain, col_rank * channels, channels, 0)

    core = lax.axis_index("core")
    scaled_pair = jnp.concatenate([scaled_full, lax.ppermute(scaled_full, "core", SWAP)], axis=0)
    hidden_pair = jnp.concatenate([hidden_pre, lax.ppermute(hidden_pre, "core", SWAP)], axis=0)
    grad_act = jnp.dot(scaled_pair, w_out_full, preferred_element_type=jnp.float32)
    grad_pair_full = (grad_act * gelu_slope(hidden_pair.astype(jnp.float32))).astype(jnp.bfloat16)
    grad_pre = grad_pair_full[:tokens]

    normed_pair = jnp.concatenate([normed_full, lax.ppermute(normed_full, "core", SWAP)], axis=0)
    grad_pair = lax.dynamic_index_in_dim(
        grad_pair_full.reshape(2 * tokens, 2, hidden // 2), core, axis=1, keepdims=False
    )
    chip_sum = lax.dot_general(
        normed_pair, grad_pair, (((0,), (0,)), ((), ())), preferred_element_type=jnp.float32
    )
    chip_ready = chip_sum.astype(jnp.bfloat16)
    chip_rows = lax.psum_scatter(chip_ready, "z", scatter_dimension=0, tiled=True)
    chip_rows = chip_rows.reshape(2, width // n_row, hidden // 2)
    own = lax.dynamic_index_in_dim(chip_rows, core, axis=0, keepdims=False)
    other = lax.ppermute(
        lax.dynamic_index_in_dim(chip_rows, 1 - core, axis=0, keepdims=False), "core", SWAP
    )
    d_w_in = jnp.where(
        core == 0, jnp.concatenate([own, other], axis=1), jnp.concatenate([other, own], axis=1)
    )

    block_n = lax.dot_general(
        w_in_full.reshape(n_col, channels, hidden),
        grad_pre,
        (((2,), (1,)), ((), ())),
        preferred_element_type=jnp.float32,
    ).astype(jnp.bfloat16)
    zhat_by_owner = jnp.transpose(zhat_full.reshape(tokens, n_col, channels), (1, 2, 0))
    weighted = block_n.astype(jnp.float32) * norm_gain.reshape(n_col, channels, 1)
    first_part = jnp.sum(weighted, axis=(0, 1))
    second_part = jnp.sum(weighted * zhat_by_owner, axis=(0, 1))
    f_hi, f_lo = split_hi_lo(first_part)
    s_hi, s_lo = split_hi_lo(second_part)
    sums = jnp.stack([f_hi, f_lo, s_hi, s_lo], axis=0)
    outgoing = jnp.concatenate([block_n, jnp.broadcast_to(sums[None], (n_col, 4, tokens))], axis=1)
    incoming = lax.all_to_all(outgoing, "col", 0, 0, tiled=True)
    grad_norm = jnp.sum(incoming[:, :channels].astype(jnp.float32), axis=0).T
    totals = jnp.sum(incoming[:, channels:].astype(jnp.float32), axis=0).T
    first = (totals[:, 0] + totals[:, 1])[:, None] / width
    second = (totals[:, 2] + totals[:, 3])[:, None] / width
    dzhat = grad_norm * gain_own
    grad_conv = (rstd * (dzhat - first - zhat_own * second)).astype(jnp.bfloat16)
    gain_part = jnp.sum(grad_norm * zhat_own, axis=0)
    bias_part = jnp.sum(grad_norm, axis=0)

    per_image = H // rows
    grid = grad_conv.reshape(rows, H, channels)
    down_pairs = [(i, i + 1) for i in range(n_row) if (i + 1) % per_image != 0]
    up_pairs = [(i + 1, i) for i in range(n_row) if (i + 1) % per_image != 0]
    from_above = lax.ppermute(grid[rows - HALO :], ROW, down_pairs)
    from_below = lax.ppermute(grid[:HALO], ROW, up_pairs)
    tall = jnp.concatenate([from_above, grid, from_below], axis=0)
    padded = jnp.pad(tall, ((0, 0), (HALO, HALO), (0, 0)))
    d_input, kernel_sums = conv_call(
        padded,
        block_input.reshape(rows, H, channels),
        cotangent.reshape(rows, H, channels),
        kernel_rows_full,
    )
    d_input = d_input.reshape(tokens, channels)

    n_chip = n_row // 2
    partials = jnp.concatenate([kernel_sums.reshape(-1), gain_part, bias_part])
    partials = partials + lax.ppermute(partials, "core", SWAP)
    kernel_chip = partials[: KS * KS * channels].reshape(KS * KS, n_chip, 2, few)
    kernel_chip = lax.dynamic_index_in_dim(kernel_chip, core, axis=2, keepdims=False)
    kernel_chip = jnp.transpose(kernel_chip, (1, 0, 2)).reshape(n_chip, KS * KS * few)
    norm_chip = jnp.broadcast_to(partials[None, KS * KS * channels :], (n_chip, 2 * channels))
    reduced = jnp.sum(
        lax.all_to_all(jnp.concatenate([kernel_chip, norm_chip], axis=1), "z", 0, 0, tiled=True),
        axis=0,
    )
    d_kernel = reduced[: KS * KS * few].reshape(KS * KS, few)
    d_gain = reduced[KS * KS * few : KS * KS * few + channels]
    d_bias = reduced[KS * KS * few + channels :]
    return (d_input, d_kernel, d_gain, d_bias, d_w_in)


def solution(mesh):
    devices = mesh.devices
    split = Mesh(devices.reshape(devices.shape[0] // 2, 2, devices.shape[1]), ROW + ("col",))
    return jax.shard_map(
        body,
        mesh=split,
        in_specs=(
            P(ROW, "col"),
            P(ROW, "col"),
            P(ROW, "col"),
            P(ROW, "col"),
            P(None, ("col",) + ROW),
            P(),
            P(),
            P("col"),
            P(ROW, "col"),
            P(ROW, "col"),
        ),
        out_specs=(P(ROW, "col"), P(None, ("col",) + ROW), P("col"), P("col"), P(ROW, "col")),
        check_vma=False,
    )
```

```python
import jax
import jax.numpy as jnp
from jax import lax
from jax.experimental import pallas as pl
from jax.experimental.pallas import tpu as pltpu
from jax.sharding import Mesh, PartitionSpec as P

KS = 7
H = 64
HALO = KS // 2

WEIGHTS_VIA = "gather"
ROW = ("z", "core")
SWAP = [(0, 1), (1, 0)]
ACTS_VIA = "a2a"


def gelu_slope(values):
    cdf = 0.5 * (1.0 + lax.erf(values * 0.7071067811865476))
    density = jnp.exp(-0.5 * values * values) * 0.3989422804014327
    return cdf + values * density


def gather_blocks(x, axis_name, size, via):
    if via == "a2a":
        wide = jnp.broadcast_to(x[None], (size,) + x.shape)
        return lax.all_to_all(wide, axis_name, 0, 0, tiled=True)
    return lax.all_gather(x, axis_name, axis=0, tiled=False)


def split_three(values):
    high = lax.reduce_precision(values, exponent_bits=8, mantissa_bits=7)
    rest = values - high
    middle = lax.reduce_precision(rest, exponent_bits=8, mantissa_bits=7)
    low = rest - middle
    return jnp.stack([high, middle, low]).astype(jnp.bfloat16)


def conv_body(tall_ref, inputs_ref, cot_ref, kernel_ref, din_ref, dk_ref, pad_ref):
    rows, span, channels = inputs_ref.shape
    pad_ref[...] = tall_ref[...].astype(jnp.float32)
    inputs = inputs_ref[...].astype(jnp.float32)
    moved = jnp.zeros((rows, span, channels), jnp.float32)
    for across in range(KS):
        slab = pad_ref[:, 2 * HALO - across : 2 * HALO - across + span, :]
        for down in range(KS):
            tap = down * KS + across
            window = slab[2 * HALO - down : 2 * HALO - down + rows]
            moved = moved + kernel_ref[tap : tap + 1, :][None] * window
            part = jnp.sum(window * inputs, axis=0).reshape(span // 8, 8, channels)
            dk_ref[tap] = jnp.sum(part, axis=0)
    din_ref[...] = (moved + cot_ref[...].astype(jnp.float32)).astype(din_ref.dtype)


def conv_call(padded, inputs, cot, kernel_full):
    rows, span, channels = inputs.shape
    din, dk = pl.pallas_call(
        conv_body,
        out_shape=(
            jax.ShapeDtypeStruct((rows, span, channels), jnp.bfloat16),
            jax.ShapeDtypeStruct((KS * KS, 8, channels), jnp.float32),
        ),
        scratch_shapes=[pltpu.VMEM(padded.shape, jnp.float32)],
    )(padded, inputs, cot, kernel_full)
    return din, jnp.sum(dk, axis=1)


def split_hi_lo(values):
    high = lax.reduce_precision(values, exponent_bits=8, mantissa_bits=7)
    low = values - high
    return high.astype(jnp.bfloat16), low.astype(jnp.bfloat16)


def body(
    block_input,
    conv_out,
    hidden_pre,
    cotangent,
    conv_kernel,
    norm_gain,
    norm_bias,
    layer_scale,
    w_in,
    w_out,
):
    tokens, channels = block_input.shape
    width = norm_gain.shape[0]
    hidden = hidden_pre.shape[1]
    n_col = width // channels
    n_row = width // w_in.shape[0]
    few = conv_kernel.shape[1]
    rows = tokens // H
    col_rank = lax.axis_index("col")
    row_rank = lax.axis_index(ROW)

    scaled = (cotangent.astype(jnp.float32) * layer_scale).astype(jnp.bfloat16)
    acts = gather_blocks(jnp.concatenate([scaled, conv_out], axis=1), "col", n_col, ACTS_VIA)
    kernel_bits = split_three(conv_kernel).reshape(-1)
    rows_extra = -(-kernel_bits.shape[0] // hidden)
    kernel_bits = jnp.pad(kernel_bits, (0, rows_extra * hidden - kernel_bits.shape[0]))
    block_rows = w_in.shape[0]
    weights = gather_blocks(
        jnp.concatenate([w_out, w_in, kernel_bits.reshape(rows_extra, hidden)], axis=0),
        ROW,
        n_row,
        WEIGHTS_VIA,
    )
    kernel_parts = weights[:, 2 * block_rows :].reshape(n_row, -1)[:, : 3 * KS * KS * few]
    kernel_parts = kernel_parts.reshape(n_row, 3, KS * KS, few).astype(jnp.float32)
    kernel_sum = kernel_parts[:, 0] + kernel_parts[:, 1] + kernel_parts[:, 2]
    kernel_rows_full = jnp.transpose(kernel_sum, (1, 0, 2)).reshape(KS * KS, n_row * few)
    scaled_full = jnp.transpose(acts[:, :, :channels], (1, 0, 2)).reshape(tokens, width)
    inputs_full = jnp.transpose(acts[:, :, channels:], (1, 0, 2)).reshape(tokens, width)
    w_out_full = weights[:, :block_rows].reshape(width, hidden)
    w_in_full = weights[:, block_rows : 2 * block_rows].reshape(width, hidden)

    values = inputs_full.astype(jnp.float32)
    mean = jnp.mean(values, axis=1, keepdims=True)
    centred = values - mean
    rstd = lax.rsqrt(jnp.mean(centred * centred, axis=1, keepdims=True) + 1e-06)
    zhat_full = centred * rstd
    normed_full = (zhat_full * norm_gain + norm_bias).astype(jnp.bfloat16)
    zhat_own = lax.dynamic_slice_in_dim(zhat_full, col_rank * channels, channels, 1)
    gain_own = lax.dynamic_slice_in_dim(norm_gain, col_rank * channels, channels, 0)

    core = lax.axis_index("core")
    scaled_pair = jnp.concatenate([scaled_full, lax.ppermute(scaled_full, "core", SWAP)], axis=0)
    hidden_pair = jnp.concatenate([hidden_pre, lax.ppermute(hidden_pre, "core", SWAP)], axis=0)
    grad_act = jnp.dot(scaled_pair, w_out_full, preferred_element_type=jnp.float32)
    grad_pair_full = (grad_act * gelu_slope(hidden_pair.astype(jnp.float32))).astype(jnp.bfloat16)
    grad_pre = grad_pair_full[:tokens]

    normed_pair = jnp.concatenate([normed_full, lax.ppermute(normed_full, "core", SWAP)], axis=0)
    grad_pair = lax.dynamic_index_in_dim(
        grad_pair_full.reshape(2 * tokens, 2, hidden // 2), core, axis=1, keepdims=False
    )
    chip_sum = lax.dot_general(
        normed_pair, grad_pair, (((0,), (0,)), ((), ())), preferred_element_type=jnp.float32
    )
    chip_ready = chip_sum.astype(jnp.bfloat16)
    chip_rows = lax.psum_scatter(chip_ready, "z", scatter_dimension=0, tiled=True)
    chip_rows = chip_rows.reshape(2, width // n_row, hidden // 2)
    own = lax.dynamic_index_in_dim(chip_rows, core, axis=0, keepdims=False)
    other = lax.ppermute(
        lax.dynamic_index_in_dim(chip_rows, 1 - core, axis=0, keepdims=False), "core", SWAP
    )
    d_w_in = jnp.where(
        core == 0, jnp.concatenate([own, other], axis=1), jnp.concatenate([other, own], axis=1)
    )

    block_n = lax.dot_general(
        w_in_full.reshape(n_col, channels, hidden),
        grad_pre,
        (((2,), (1,)), ((), ())),
        preferred_element_type=jnp.float32,
    ).astype(jnp.bfloat16)
    zhat_by_owner = jnp.transpose(zhat_full.reshape(tokens, n_col, channels), (1, 2, 0))
    weighted = block_n.astype(jnp.float32) * norm_gain.reshape(n_col, channels, 1)
    first_part = jnp.sum(weighted, axis=(0, 1))
    second_part = jnp.sum(weighted * zhat_by_owner, axis=(0, 1))
    f_hi, f_lo = split_hi_lo(first_part)
    s_hi, s_lo = split_hi_lo(second_part)
    sums = jnp.stack([f_hi, f_lo, s_hi, s_lo], axis=0)
    outgoing = jnp.concatenate([block_n, jnp.broadcast_to(sums[None], (n_col, 4, tokens))], axis=1)
    incoming = lax.all_to_all(outgoing, "col", 0, 0, tiled=True)
    grad_norm = jnp.sum(incoming[:, :channels].astype(jnp.float32), axis=0).T
    totals = jnp.sum(incoming[:, channels:].astype(jnp.float32), axis=0).T
    first = (totals[:, 0] + totals[:, 1])[:, None] / width
    second = (totals[:, 2] + totals[:, 3])[:, None] / width
    dzhat = grad_norm * gain_own
    grad_conv = (rstd * (dzhat - first - zhat_own * second)).astype(jnp.bfloat16)
    gain_part = jnp.sum(grad_norm * zhat_own, axis=0)
    bias_part = jnp.sum(grad_norm, axis=0)

    per_image = H // rows
    grid = grad_conv.reshape(rows, H, channels)
    down_pairs = [(i, i + 1) for i in range(n_row) if (i + 1) % per_image != 0]
    up_pairs = [(i + 1, i) for i in range(n_row) if (i + 1) % per_image != 0]
    from_above = lax.ppermute(grid[rows - HALO :], ROW, down_pairs)
    from_below = lax.ppermute(grid[:HALO], ROW, up_pairs)
    tall = jnp.concatenate([from_above, grid, from_below], axis=0)
    padded = jnp.pad(tall, ((0, 0), (HALO, HALO), (0, 0)))
    d_input, kernel_sums = conv_call(
        padded,
        block_input.reshape(rows, H, channels),
        cotangent.reshape(rows, H, channels),
        kernel_rows_full,
    )
    d_input = d_input.reshape(tokens, channels)

    n_chip = n_row // 2
    partials = jnp.concatenate([kernel_sums.reshape(-1), gain_part, bias_part])
    partials = partials + lax.ppermute(partials, "core", SWAP)
    kernel_chip = partials[: KS * KS * channels].reshape(KS * KS, n_chip, 2, few)
    kernel_chip = lax.dynamic_index_in_dim(kernel_chip, core, axis=2, keepdims=False)
    kernel_chip = jnp.transpose(kernel_chip, (1, 0, 2)).reshape(n_chip, KS * KS * few)
    norm_chip = jnp.broadcast_to(partials[None, KS * KS * channels :], (n_chip, 2 * channels))
    reduced = jnp.sum(
        lax.all_to_all(jnp.concatenate([kernel_chip, norm_chip], axis=1), "z", 0, 0, tiled=True),
        axis=0,
    )
    d_kernel = reduced[: KS * KS * few].reshape(KS * KS, few)
    d_gain = reduced[KS * KS * few : KS * KS * few + channels]
    d_bias = reduced[KS * KS * few + channels :]
    return (d_input, d_kernel, d_gain, d_bias, d_w_in)


def solution(mesh):
    devices = mesh.devices
    split = Mesh(devices.reshape(devices.shape[0] // 2, 2, devices.shape[1]), ROW + ("col",))
    return jax.shard_map(
        body,
        mesh=split,
        in_specs=(
            P(ROW, "col"),
            P(ROW, "col"),
            P(ROW, "col"),
            P(ROW, "col"),
            P(None, ("col",) + ROW),
            P(),
            P(),
            P("col"),
            P(ROW, "col"),
            P(ROW, "col"),
        ),
        out_specs=(P(ROW, "col"), P(None, ("col",) + ROW), P("col"), P("col"), P(ROW, "col")),
        check_vma=False,
    )
```

```python
import jax
import jax.numpy as jnp
from jax import lax
from jax.experimental import pallas as pl
from jax.experimental.pallas import tpu as pltpu
from jax.sharding import Mesh, PartitionSpec as P

KS = 7
H = 64
HALO = KS // 2

WEIGHTS_VIA = "gather"
ROW = ("z", "core")
SWAP = [(0, 1), (1, 0)]
ACTS_VIA = "a2a"


def gelu_slope(values):
    cdf = 0.5 * (1.0 + lax.erf(values * 0.7071067811865476))
    density = jnp.exp(-0.5 * values * values) * 0.3989422804014327
    return cdf + values * density


def gather_blocks(x, axis_name, size, via):
    if via == "a2a":
        wide = jnp.broadcast_to(x[None], (size,) + x.shape)
        return lax.all_to_all(wide, axis_name, 0, 0, tiled=True)
    return lax.all_gather(x, axis_name, axis=0, tiled=False)


def split_three(values):
    high = lax.reduce_precision(values, exponent_bits=8, mantissa_bits=7)
    rest = values - high
    middle = lax.reduce_precision(rest, exponent_bits=8, mantissa_bits=7)
    low = rest - middle
    return jnp.stack([high, middle, low]).astype(jnp.bfloat16)


def conv_body(tall_ref, inputs_ref, cot_ref, kernel_ref, din_ref, dk_ref, pad_ref):
    rows, span, channels = inputs_ref.shape
    pad_ref[...] = tall_ref[...].astype(jnp.float32)
    inputs = inputs_ref[...].astype(jnp.float32)
    moved = jnp.zeros((rows, span, channels), jnp.float32)
    for across in range(KS):
        slab = pad_ref[:, 2 * HALO - across : 2 * HALO - across + span, :]
        for down in range(KS):
            tap = down * KS + across
            window = slab[2 * HALO - down : 2 * HALO - down + rows]
            moved = moved + kernel_ref[tap : tap + 1, :][None] * window
            part = jnp.sum(window * inputs, axis=0).reshape(span // 8, 8, channels)
            dk_ref[tap] = jnp.sum(part, axis=0)
    din_ref[...] = (moved + cot_ref[...].astype(jnp.float32)).astype(din_ref.dtype)


def conv_call(padded, inputs, cot, kernel_full):
    rows, span, channels = inputs.shape
    din, dk = pl.pallas_call(
        conv_body,
        out_shape=(
            jax.ShapeDtypeStruct((rows, span, channels), jnp.bfloat16),
            jax.ShapeDtypeStruct((KS * KS, 8, channels), jnp.float32),
        ),
        scratch_shapes=[pltpu.VMEM(padded.shape, jnp.float32)],
    )(padded, inputs, cot, kernel_full)
    return din, jnp.sum(dk, axis=1)


def split_hi_lo(values):
    high = lax.reduce_precision(values, exponent_bits=8, mantissa_bits=7)
    low = values - high
    return high.astype(jnp.bfloat16), low.astype(jnp.bfloat16)


def body(
    block_input,
    conv_out,
    hidden_pre,
    cotangent,
    conv_kernel,
    norm_gain,
    norm_bias,
    layer_scale,
    w_in,
    w_out,
):
    tokens, channels = block_input.shape
    width = norm_gain.shape[0]
    hidden = hidden_pre.shape[1]
    n_col = width // channels
    n_row = width // w_in.shape[0]
    few = conv_kernel.shape[1]
    rows = tokens // H
    col_rank = lax.axis_index("col")
    row_rank = lax.axis_index(ROW)

    scaled = (cotangent.astype(jnp.float32) * layer_scale).astype(jnp.bfloat16)
    acts = gather_blocks(jnp.concatenate([scaled, conv_out], axis=1), "col", n_col, ACTS_VIA)
    kernel_bits = split_three(conv_kernel).reshape(-1)
    rows_extra = -(-kernel_bits.shape[0] // hidden)
    kernel_bits = jnp.pad(kernel_bits, (0, rows_extra * hidden - kernel_bits.shape[0]))
    block_rows = w_in.shape[0]
    weights = gather_blocks(
        jnp.concatenate([w_out, w_in, kernel_bits.reshape(rows_extra, hidden)], axis=0),
        ROW,
        n_row,
        WEIGHTS_VIA,
    )
    kernel_parts = weights[:, 2 * block_rows :].reshape(n_row, -1)[:, : 3 * KS * KS * few]
    kernel_parts = kernel_parts.reshape(n_row, 3, KS * KS, few).astype(jnp.float32)
    kernel_sum = kernel_parts[:, 0] + kernel_parts[:, 1] + kernel_parts[:, 2]
    kernel_rows_full = jnp.transpose(kernel_sum, (1, 0, 2)).reshape(KS * KS, n_row * few)
    scaled_full = jnp.transpose(acts[:, :, :channels], (1, 0, 2)).reshape(tokens, width)
    inputs_full = jnp.transpose(acts[:, :, channels:], (1, 0, 2)).reshape(tokens, width)
    w_out_full = weights[:, :block_rows].reshape(width, hidden)
    w_in_full = weights[:, block_rows : 2 * block_rows].reshape(width, hidden)

    values = inputs_full.astype(jnp.float32)
    mean = jnp.mean(values, axis=1, keepdims=True)
    centred = values - mean
    rstd = lax.rsqrt(jnp.mean(centred * centred, axis=1, keepdims=True) + 1e-06)
    zhat_full = centred * rstd
    normed_full = (zhat_full * norm_gain + norm_bias).astype(jnp.bfloat16)
    zhat_own = lax.dynamic_slice_in_dim(zhat_full, col_rank * channels, channels, 1)
    gain_own = lax.dynamic_slice_in_dim(norm_gain, col_rank * channels, channels, 0)

    core = lax.axis_index("core")
    scaled_pair = jnp.concatenate([scaled_full, lax.ppermute(scaled_full, "core", SWAP)], axis=0)
    hidden_pair = jnp.concatenate([hidden_pre, lax.ppermute(hidden_pre, "core", SWAP)], axis=0)
    grad_act = jnp.dot(scaled_pair, w_out_full, preferred_element_type=jnp.float32)
    grad_pair_full = (grad_act * gelu_slope(hidden_pair.astype(jnp.float32))).astype(jnp.bfloat16)
    grad_pre = grad_pair_full[:tokens]

    normed_pair = jnp.concatenate([normed_full, lax.ppermute(normed_full, "core", SWAP)], axis=0)
    grad_pair = lax.dynamic_index_in_dim(
        grad_pair_full.reshape(2 * tokens, 2, hidden // 2), core, axis=1, keepdims=False
    )
    chip_sum = lax.dot_general(
        normed_pair, grad_pair, (((0,), (0,)), ((), ())), preferred_element_type=jnp.float32
    )
    chip_ready = chip_sum.astype(jnp.bfloat16)
    chip_rows = lax.psum_scatter(chip_ready, "z", scatter_dimension=0, tiled=True)
    chip_rows = chip_rows.reshape(2, width // n_row, hidden // 2)
    own = lax.dynamic_index_in_dim(chip_rows, core, axis=0, keepdims=False)
    other = lax.ppermute(
        lax.dynamic_index_in_dim(chip_rows, 1 - core, axis=0, keepdims=False), "core", SWAP
    )
    d_w_in = jnp.where(
        core == 0, jnp.concatenate([own, other], axis=1), jnp.concatenate([other, own], axis=1)
    )

    block_n = lax.dot_general(
        w_in_full.reshape(n_col, channels, hidden),
        grad_pre,
        (((2,), (1,)), ((), ())),
        preferred_element_type=jnp.float32,
    ).astype(jnp.bfloat16)
    zhat_by_owner = jnp.transpose(zhat_full.reshape(tokens, n_col, channels), (1, 2, 0))
    weighted = block_n.astype(jnp.float32) * norm_gain.reshape(n_col, channels, 1)
    first_part = jnp.sum(weighted, axis=(0, 1))
    second_part = jnp.sum(weighted * zhat_by_owner, axis=(0, 1))
    f_hi, f_lo = split_hi_lo(first_part)
    s_hi, s_lo = split_hi_lo(second_part)
    sums = jnp.stack([f_hi, f_lo, s_hi, s_lo], axis=0)
    outgoing = jnp.concatenate([block_n, jnp.broadcast_to(sums[None], (n_col, 4, tokens))], axis=1)
    incoming = lax.all_to_all(outgoing, "col", 0, 0, tiled=True)
    grad_norm = jnp.sum(incoming[:, :channels].astype(jnp.float32), axis=0).T
    totals = jnp.sum(incoming[:, channels:].astype(jnp.float32), axis=0).T
    first = (totals[:, 0] + totals[:, 1])[:, None] / width
    second = (totals[:, 2] + totals[:, 3])[:, None] / width
    dzhat = grad_norm * gain_own
    grad_conv = (rstd * (dzhat - first - zhat_own * second)).astype(jnp.bfloat16)
    gain_part = jnp.sum(grad_norm * zhat_own, axis=0)
    bias_part = jnp.sum(grad_norm, axis=0)

    per_image = H // rows
    grid = grad_conv.reshape(rows, H, channels)
    down_pairs = [(i, i + 1) for i in range(n_row) if (i + 1) % per_image != 0]
    up_pairs = [(i + 1, i) for i in range(n_row) if (i + 1) % per_image != 0]
    from_above = lax.ppermute(grid[rows - HALO :], ROW, down_pairs)
    from_below = lax.ppermute(grid[:HALO], ROW, up_pairs)
    tall = jnp.concatenate([from_above, grid, from_below], axis=0)
    padded = jnp.pad(tall, ((0, 0), (HALO, HALO), (0, 0)))
    d_input, kernel_sums = conv_call(
        padded,
        block_input.reshape(rows, H, channels),
        cotangent.reshape(rows, H, channels),
        kernel_rows_full,
    )
    d_input = d_input.reshape(tokens, channels)

    n_chip = n_row // 2
    partials = jnp.concatenate([kernel_sums.reshape(-1), gain_part, bias_part])
    partials = partials + lax.ppermute(partials, "core", SWAP)
    step = 1
    while step < n_chip:
        partials = partials + lax.ppermute(partials, "z", [(i, i ^ step) for i in range(n_chip)])
        step *= 2
    kernel_total = partials[: KS * KS * channels].reshape(KS * KS, channels)
    d_kernel = lax.dynamic_slice_in_dim(kernel_total, row_rank * few, few, 1)
    d_gain = partials[KS * KS * channels : KS * KS * channels + channels]
    d_bias = partials[KS * KS * channels + channels :]
    return (d_input, d_kernel, d_gain, d_bias, d_w_in)


def solution(mesh):
    devices = mesh.devices
    split = Mesh(devices.reshape(devices.shape[0] // 2, 2, devices.shape[1]), ROW + ("col",))
    return jax.shard_map(
        body,
        mesh=split,
        in_specs=(
            P(ROW, "col"),
            P(ROW, "col"),
            P(ROW, "col"),
            P(ROW, "col"),
            P(None, ("col",) + ROW),
            P(),
            P(),
            P("col"),
            P(ROW, "col"),
            P(ROW, "col"),
        ),
        out_specs=(P(ROW, "col"), P(None, ("col",) + ROW), P("col"), P("col"), P(ROW, "col")),
        check_vma=False,
    )
```
